32 devices in a mesh: section: 2 (over core), latent: 4 (over z), tok: 4 (over y, x).
Axes of the slice: x: 2, y: 2, z: 4, core: 2. Of those that a mesh axis runs over, the one named last changes fastest.
Arguments:
- acts: bfloat16 [2, 256, 8192], P('section', 'latent', 'tok'), may hold values from -6 to 6
- enc_weight: bfloat16 [2, 8192, 32768], P('section', 'tok', 'latent'), may hold values from -0.046875 to 0.046875
- enc_bias: float32 [32768], P('latent'), may hold values from -3 to 3
- dec_weight: bfloat16 [32768, 2, 8192], P('latent', 'section', 'tok'), may hold values from -0.15625 to 0.15625
- dec_bias: float32 [2, 8192], P('section', 'tok'), may hold values from -3 to 3
- active_blocks: int32 [2, 32], replicated, may hold values from 0 to 255, as said below
- block_counts: int32 [2], replicated, may hold values from 16 to 32
Outputs:
- rebuilt: bfloat16 [2, 256, 8192], P('section', 'latent', 'tok')
The draws below stay inside these ranges and needn't reach their ends.
Inputs may be any that keep to these rules, and one draw needn't show every extreme that they name: `active_blocks`: within a tile the 32 listed ids are distinct; entries past the tile's count are ignored.
All inputs are finite; a program needn't handle non-finite values.
Results may differ from the reference program's by a relative error of at most 0.0048.
Values may be sent and summed in bfloat16 or wider, within the bound.
No kernel may reach another device: no remote copies, remote signals or barrier semaphores. Data moves between devices by JAX's collectives and lax.ppermute only.
A program may use at most 128 MiB of HBM per device.

```python
import jax
import jax.numpy as jnp

D = 8192
LATENTS = 32768
BLOCK = 128
TILE = 128
MOSTB = 32
TOKENS = 256
LAYERS = 2
NBLOCKS = 256
NTILES = 2


def active_pair(key):
    base = jax.random.fold_in(key, 11)
    key_warm, key_jitter, key_count, key_fullest = jax.random.split(base, 4)
    warmth = jax.random.randint(key_warm, (NBLOCKS,), 0, 3)
    jitter = jax.random.randint(key_jitter, (NTILES, NBLOCKS), 0, NBLOCKS)
    ranking = (jitter + warmth[None, :] * (NBLOCKS // 2)) * NBLOCKS + jnp.arange(NBLOCKS, dtype=jnp.int32)[None, :]
    chosen = jnp.argsort(-ranking, axis=1, stable=True)[:, :MOSTB].astype(jnp.int32)
    counts = jax.random.randint(key_count, (NTILES,), MOSTB // 2, MOSTB + 1)
    fullest = jax.random.randint(key_fullest, (), 0, NTILES)
    tile_ids = jnp.arange(NTILES, dtype=jnp.int32)
    counts = jnp.where(tile_ids == fullest, MOSTB, counts)
    counts = jnp.where(tile_ids == (fullest + 1) % NTILES, MOSTB // 2, counts)
    return (chosen, counts.astype(jnp.int32))


def draw_active_blocks(key, part):
    return active_pair(key)[0]


def draw_block_counts(key, part):
    return active_pair(key)[1]


def shard_levels(stream_key, extent, cuts, smallest, high):
    loudness, own = 1.0, jax.random.fold_in(stream_key, 6)
    for axis_at, parts in cuts:
        heights = jnp.exp(jax.random.uniform(jax.random.fold_in(own, axis_at), (parts,), jnp.float32, smallest / len(cuts), high / len(cuts)))
        loudness = loudness * jnp.repeat(heights, extent[axis_at] // parts).reshape([-1 if axis == axis_at else 1 for axis in range(len(extent))])
    return loudness


def scatter_about(own_key, dims, deviation, reach, cuts=(), kind=jnp.bfloat16):
    gain = shard_levels(own_key, dims, cuts, -0.22, 0.18) if cuts else 1.0
    array = jax.random.normal(own_key, dims, jnp.float32) * deviation * gain
    return jnp.minimum(jnp.maximum(array, -reach), reach).astype(kind)


def setup_inputs(seed: int = 0) -> dict:
    key_list = jax.random.split(jax.random.key(seed), 8)
    acts = scatter_about(key_list[0], (LAYERS, TOKENS, D), 1.0, 6.0, ((0, 2), (1, 4), (2, 4)))
    enc_weight = scatter_about(key_list[1], (LAYERS, D, LATENTS), (2 * D) ** -0.5, 0.046875, ((0, 2), (1, 4), (2, 4)))
    enc_bias = scatter_about(key_list[2], (LATENTS,), 0.5, 3.0, ((0, 4),), jnp.float32)
    dec_weight = scatter_about(key_list[3], (LATENTS, LAYERS, D), (MOSTB * 48) ** -0.5, 0.15625, ((0, 4), (1, 2), (2, 4)))
    dec_bias = scatter_about(key_list[4], (LAYERS, D), 0.5, 3.0, ((0, 2), (1, 4)), jnp.float32)
    active_blocks = draw_active_blocks(jax.random.fold_in(key_list[7], 71), 0)
    block_counts = draw_block_counts(jax.random.fold_in(key_list[7], 71), 0)
    return dict(acts=acts, enc_weight=enc_weight, enc_bias=enc_bias, dec_weight=dec_weight, dec_bias=dec_bias, active_blocks=active_blocks, block_counts=block_counts)


def block_table(active_blocks, block_counts):
    slot_ids = jnp.arange(MOSTB, dtype=jnp.int32)
    in_list = slot_ids[None, :] < block_counts[:, None]
    all_blocks = jnp.arange(NBLOCKS, dtype=jnp.int32)
    matches = (active_blocks[:, :, None] == all_blocks[None, None, :]) & in_list[:, :, None]
    return jnp.any(matches, axis=1).astype(jnp.float32)


def reference(acts, enc_weight, enc_bias, dec_weight, dec_bias, active_blocks, block_counts):
    preact = jnp.zeros((TOKENS, LATENTS), jnp.float32)
    for depth_index in range(LAYERS):
        preact = preact + jnp.dot(acts[depth_index], enc_weight[depth_index], preferred_element_type=jnp.float32)
    block_mask = block_table(active_blocks, block_counts)
    latent_mask = jnp.repeat(jnp.repeat(block_mask, TILE, axis=0), BLOCK, axis=1)
    latent_codes = (jax.nn.relu(preact + enc_bias[None, :]) * latent_mask).astype(jnp.bfloat16)
    outputs = []
    for depth_index in range(LAYERS):
        product = jnp.dot(latent_codes, dec_weight[:, depth_index, :], preferred_element_type=jnp.float32)
        outputs.append((product + dec_bias[depth_index][None, :]).astype(jnp.bfloat16))
    return jnp.stack(outputs, axis=0)
```

```python
import jax
import jax.numpy as jnp
from jax import lax
from jax.sharding import PartitionSpec as P

BLOCK = 128
TILE = 128


def slot_table(active_blocks, block_counts, first_block, blocks_local, slots):
    listed = active_blocks.shape[1]
    slot_ids = jnp.arange(listed, dtype=jnp.int32)
    local = active_blocks - first_block
    valid = (slot_ids[None, :] < block_counts[:, None]) & (local >= 0) & (local < blocks_local)
    order = jnp.argsort(jnp.logical_not(valid).astype(jnp.int32), axis=1, stable=True)[:, :slots]
    picked_valid = jnp.take_along_axis(valid, order, axis=1)
    picked = jnp.where(picked_valid, jnp.take_along_axis(local, order, axis=1), 0)
    return picked, picked_valid


def shards(acts, enc_weight, enc_bias, dec_weight, dec_bias, active_blocks, block_counts):
    local_enc = enc_weight[0]
    tokens_all = lax.all_gather(acts, "latent", axis=1, tiled=True)[0]
    preact = jnp.dot(tokens_all, local_enc, preferred_element_type=jnp.float32)
    n_tok, n_lat = preact.shape
    tiles = n_tok // TILE
    blocks_local = n_lat // BLOCK
    slots = min(active_blocks.shape[1], blocks_local)
    first_block = lax.axis_index("latent") * blocks_local
    picked, picked_valid = slot_table(active_blocks, block_counts, first_block, blocks_local, slots)

    tiled_pre = preact.reshape(tiles, TILE, blocks_local, BLOCK)
    compact = jax.vmap(lambda p, i: p[:, i, :])(tiled_pre, picked)
    shared = lax.psum_scatter(compact, ("section", "tok"), scatter_dimension=1, tiled=True)
    bias_slots = enc_bias.reshape(blocks_local, BLOCK)[picked]
    keep = picked_valid.astype(jnp.float32)[:, None, :, None]
    codes_part = (jax.nn.relu(shared + bias_slots[:, None, :, :]) * keep).astype(jnp.bfloat16)
    codes_compact = lax.all_gather(codes_part, ("section", "tok"), axis=1, tiled=True)

    dense = jnp.zeros((tiles, TILE, blocks_local, BLOCK), jnp.bfloat16)
    dense = jax.vmap(lambda d, i, c: d.at[:, i, :].add(c))(dense, picked, codes_compact)
    latent_codes = dense.reshape(n_tok, n_lat)

    local_dec = dec_weight[:, 0, :]
    rebuilt = lax.psum_scatter(
        jnp.dot(latent_codes, local_dec, preferred_element_type=jnp.float32),
        "latent",
        scatter_dimension=0,
        tiled=True,
    )
    return (rebuilt + dec_bias).astype(jnp.bfloat16)[None]


def solution(mesh):
    placed = (
        P("section", "latent", "tok"),
        P("section", "tok", "latent"),
        P("latent"),
        P("latent", "section", "tok"),
        P("section", "tok"),
        P(),
        P(),
    )
    return jax.shard_map(
        shards, mesh=mesh, in_specs=placed, out_specs=P("section", "latent", "tok"), check_vma=False
    )
```

```python
import functools

import jax
import jax.numpy as jnp
from jax import lax
from jax.experimental import pallas as pl
from jax.experimental.pallas import tpu as pltpu
from jax.sharding import PartitionSpec as P

BLOCK = 128
TILE = 128


def slot_table(active_blocks, block_counts, first_block, blocks_local, slots):
    listed = active_blocks.shape[1]
    slot_ids = jnp.arange(listed, dtype=jnp.int32)
    local = active_blocks - first_block
    valid = (slot_ids[None, :] < block_counts[:, None]) & (local >= 0) & (local < blocks_local)
    order = jnp.argsort(jnp.logical_not(valid).astype(jnp.int32), axis=1, stable=True)[:, :slots]
    picked_valid = jnp.take_along_axis(valid, order, axis=1)
    picked = jnp.where(picked_valid, jnp.take_along_axis(local, order, axis=1), 0)
    flat_valid = picked_valid.reshape(-1)
    flat_order = jnp.argsort(jnp.logical_not(flat_valid).astype(jnp.int32), stable=True).astype(jnp.int32)
    flat_blocks = picked.reshape(-1)[flat_order]
    count = jnp.sum(flat_valid.astype(jnp.int32)).reshape(1)
    return picked_valid, count, flat_order, flat_blocks


def encode_kernel(n_ref, slot_ref, blk_ref, acts_ref, enc_hbm, out_ref, buf, sem):
    slots = out_ref.shape[1]
    out_ref[...] = jnp.zeros(out_ref.shape, out_ref.dtype)
    n = n_ref[0]

    def copy(i, slot):
        col = pl.multiple_of(blk_ref[i] * BLOCK, BLOCK)
        return pltpu.make_async_copy(enc_hbm.at[:, pl.ds(col, BLOCK)], buf.at[slot], sem.at[slot])

    @pl.when(n > 0)
    def _():
        copy(0, 0).start()

    def body(i, carry):
        slot = i % 2
        copy(i, slot).wait()

        @pl.when(i + 1 < n)
        def _():
            copy(i + 1, 1 - slot).start()

        s = slot_ref[i]
        t = s // slots
        k = s % slots
        rows = acts_ref[pl.ds(pl.multiple_of(t * TILE, TILE), TILE), :]
        out_ref[t, k] = jnp.dot(rows, buf[slot], preferred_element_type=jnp.float32)
        return carry

    lax.fori_loop(0, n, body, 0)


def decode_kernel(n_ref, slot_ref, blk_ref, codes_ref, dec_hbm, out_ref, buf, sem):
    slots = codes_ref.shape[1]
    out_ref[...] = jnp.zeros(out_ref.shape, out_ref.dtype)
    n = n_ref[0]

    def copy(i, slot):
        row = pl.multiple_of(blk_ref[i] * BLOCK, BLOCK)
        return pltpu.make_async_copy(dec_hbm.at[pl.ds(row, BLOCK), :], buf.at[slot], sem.at[slot])

    @pl.when(n > 0)
    def _():
        copy(0, 0).start()

    def body(i, carry):
        slot = i % 2
        copy(i, slot).wait()

        @pl.when(i + 1 < n)
        def _():
            copy(i + 1, 1 - slot).start()

        s = slot_ref[i]
        t = s // slots
        k = s % slots
        rows = pl.ds(pl.multiple_of(t * TILE, TILE), TILE)
        out_ref[rows, :] += jnp.dot(codes_ref[t, k], buf[slot], preferred_element_type=jnp.float32)
        return carry

    lax.fori_loop(0, n, body, 0)


def sparse_call(kernel, out_shape, buf_shape, count, flat_order, flat_blocks, dense, weight, flops, nbytes):
    smem = pl.BlockSpec(memory_space=pltpu.SMEM)
    return pl.pallas_call(
        kernel,
        out_shape=out_shape,
        in_specs=[smem, smem, smem, pl.BlockSpec(memory_space=pltpu.VMEM), pl.BlockSpec(memory_space=pl.ANY)],
        out_specs=pl.BlockSpec(memory_space=pltpu.VMEM),
        scratch_shapes=[pltpu.VMEM(buf_shape, weight.dtype), pltpu.SemaphoreType.DMA((2,))],
        cost_estimate=pl.CostEstimate(flops=flops, bytes_accessed=nbytes, transcendentals=0),
    )(count, flat_order, flat_blocks, dense, weight)


def shards(acts, enc_weight, enc_bias, dec_weight, dec_bias, active_blocks, block_counts):
    local_enc = enc_weight[0]
    local_dec = dec_weight[:, 0, :]
    width, n_lat = local_enc.shape
    tokens_all = lax.all_gather(acts, "latent", axis=1, tiled=True)[0]
    n_tok = tokens_all.shape[0]
    tiles = n_tok // TILE
    blocks_local = n_lat // BLOCK
    slots = min(active_blocks.shape[1], blocks_local)
    first_block = lax.axis_index("latent") * blocks_local
    picked_valid, count, flat_order, flat_blocks = slot_table(
        active_blocks, block_counts, first_block, blocks_local, slots
    )
    pairs = tiles * slots

    compact = sparse_call(
        encode_kernel,
        jax.ShapeDtypeStruct((tiles, slots, TILE, BLOCK), jnp.float32),
        (2, width, BLOCK),
        count, flat_order, flat_blocks, tokens_all, local_enc,
        2 * pairs * TILE * width * BLOCK, pairs * (width * BLOCK * 2 + TILE * BLOCK * 4),
    )
    shared = lax.psum_scatter(compact, ("section", "tok"), scatter_dimension=2, tiled=True)
    bias_slots = enc_bias.reshape(blocks_local, BLOCK)
    slot_blocks = jnp.zeros((tiles * slots,), jnp.int32).at[flat_order].set(flat_blocks).reshape(tiles, slots)
    bias_slots = bias_slots[slot_blocks]
    codes_part = jnp.where(
        picked_valid[:, :, None, None], jax.nn.relu(shared + bias_slots[:, :, None, :]), 0.0
    ).astype(jnp.bfloat16)
    codes = lax.all_gather(codes_part, ("section", "tok"), axis=2, tiled=True)

    partial = sparse_call(
        decode_kernel,
        jax.ShapeDtypeStruct((n_tok, local_dec.shape[1]), jnp.float32),
        (2, BLOCK, local_dec.shape[1]),
        count, flat_order, flat_blocks, codes, local_dec,
        2 * pairs * TILE * BLOCK * local_dec.shape[1], pairs * BLOCK * local_dec.shape[1] * 2,
    )
    rebuilt = lax.psum_scatter(partial, "latent", scatter_dimension=0, tiled=True)
    return (rebuilt + dec_bias).astype(jnp.bfloat16)[None]


def solution(mesh):
    placed = (
        P("section", "latent", "tok"),
        P("section", "tok", "latent"),
        P("latent"),
        P("latent", "section", "tok"),
        P("section", "tok"),
        P(),
        P(),
    )
    return jax.shard_map(
        shards, mesh=mesh, in_specs=placed, out_specs=P("section", "latent", "tok"), check_vma=False
    )
```

```python
import functools

import jax
import jax.numpy as jnp
from jax import lax
from jax.experimental import pallas as pl
from jax.experimental.pallas import tpu as pltpu
from jax.sharding import PartitionSpec as P

BLOCK = 128
TILE = 128


def slot_table(active_blocks, block_counts, first_block, blocks_local, slots):
    listed = active_blocks.shape[1]
    slot_ids = jnp.arange(listed, dtype=jnp.int32)
    local = active_blocks - first_block
    valid = (slot_ids[None, :] < block_counts[:, None]) & (local >= 0) & (local < blocks_local)
    order = jnp.argsort(jnp.logical_not(valid).astype(jnp.int32), axis=1, stable=True)[:, :slots]
    picked_valid = jnp.take_along_axis(valid, order, axis=1)
    picked = jnp.where(picked_valid, jnp.take_along_axis(local, order, axis=1), 0)
    flat_valid = picked_valid.reshape(-1)
    flat_order = jnp.argsort(jnp.logical_not(flat_valid).astype(jnp.int32), stable=True).astype(jnp.int32)
    flat_blocks = picked.reshape(-1)[flat_order]
    count = jnp.sum(flat_valid.astype(jnp.int32)).reshape(1)
    return picked_valid, count, flat_order, flat_blocks


DEPTH = 6


def weight_stream(n, blk_ref, source, buf, sem, compute):
    def copy(i, slot):
        return pltpu.make_async_copy(source(blk_ref[i]), buf.at[slot], sem.at[slot])

    for j in range(DEPTH):
        @pl.when(j < n)
        def _():
            copy(j, j).start()

    def body(i, carry):
        slot = i % DEPTH
        copy(i, slot).wait()
        compute(i, buf.at[slot])

        @pl.when(i + DEPTH < n)
        def _():
            copy(i + DEPTH, slot).start()

        return carry

    lax.fori_loop(0, n, body, 0)


def encode_kernel(n_ref, slot_ref, blk_ref, acts_ref, enc_hbm, out_ref, buf, sem):
    slots = out_ref.shape[1]
    out_ref[...] = jnp.zeros(out_ref.shape, out_ref.dtype)

    def source(b):
        return enc_hbm.at[:, pl.ds(pl.multiple_of(b * BLOCK, BLOCK), BLOCK)]

    def compute(i, block):
        s = slot_ref[i]
        t = s // slots
        k = s % slots
        rows = acts_ref[pl.ds(pl.multiple_of(t * TILE, TILE), TILE), :]
        out_ref[t, k] = jnp.dot(rows, block[...], preferred_element_type=jnp.float32)

    weight_stream(n_ref[0], blk_ref, source, buf, sem, compute)


def decode_kernel(n_ref, slot_ref, blk_ref, codes_ref, dec_hbm, out_ref, buf, sem):
    slots = codes_ref.shape[1]
    out_ref[...] = jnp.zeros(out_ref.shape, out_ref.dtype)

    def source(b):
        return dec_hbm.at[pl.ds(pl.multiple_of(b * BLOCK, BLOCK), BLOCK), :]

    def compute(i, block):
        s = slot_ref[i]
        t = s // slots
        k = s % slots
        rows = pl.ds(pl.multiple_of(t * TILE, TILE), TILE)
        out_ref[rows, :] += jnp.dot(codes_ref[t, k], block[...], preferred_element_type=jnp.float32)

    weight_stream(n_ref[0], blk_ref, source, buf, sem, compute)


def sparse_call(kernel, out_shape, buf_shape, count, flat_order, flat_blocks, dense, weight, flops, nbytes):
    smem = pl.BlockSpec(memory_space=pltpu.SMEM)
    return pl.pallas_call(
        kernel,
        out_shape=out_shape,
        in_specs=[smem, smem, smem, pl.BlockSpec(memory_space=pltpu.VMEM), pl.BlockSpec(memory_space=pl.ANY)],
        out_specs=pl.BlockSpec(memory_space=pltpu.VMEM),
        scratch_shapes=[pltpu.VMEM((DEPTH,) + buf_shape, weight.dtype), pltpu.SemaphoreType.DMA((DEPTH,))],
        cost_estimate=pl.CostEstimate(flops=flops, bytes_accessed=nbytes, transcendentals=0),
    )(count, flat_order, flat_blocks, dense, weight)


def shards(acts, enc_weight, enc_bias, dec_weight, dec_bias, active_blocks, block_counts):
    local_enc = enc_weight[0]
    local_dec = dec_weight[:, 0, :]
    width, n_lat = local_enc.shape
    tokens_all = lax.all_gather(acts, "latent", axis=1, tiled=True)[0]
    n_tok = tokens_all.shape[0]
    tiles = n_tok // TILE
    blocks_local = n_lat // BLOCK
    slots = min(active_blocks.shape[1], blocks_local)
    first_block = lax.axis_index("latent") * blocks_local
    picked_valid, count, flat_order, flat_blocks = slot_table(
        active_blocks, block_counts, first_block, blocks_local, slots
    )
    pairs = tiles * slots

    compact = sparse_call(
        encode_kernel,
        jax.ShapeDtypeStruct((tiles, slots, TILE, BLOCK), jnp.float32),
        (width, BLOCK),
        count, flat_order, flat_blocks, tokens_all, local_enc,
        2 * pairs * TILE * width * BLOCK, pairs * (width * BLOCK * 2 + TILE * BLOCK * 4),
    )
    shared = lax.psum_scatter(compact, ("section", "tok"), scatter_dimension=2, tiled=True)
    bias_slots = enc_bias.reshape(blocks_local, BLOCK)
    slot_blocks = jnp.zeros((tiles * slots,), jnp.int32).at[flat_order].set(flat_blocks).reshape(tiles, slots)
    bias_slots = bias_slots[slot_blocks]
    codes_part = jnp.where(
        picked_valid[:, :, None, None], jax.nn.relu(shared + bias_slots[:, :, None, :]), 0.0
    ).astype(jnp.bfloat16)
    codes = lax.all_gather(codes_part, ("section", "tok"), axis=2, tiled=True)

    partial = sparse_call(
        decode_kernel,
        jax.ShapeDtypeStruct((n_tok, local_dec.shape[1]), jnp.float32),
        (BLOCK, local_dec.shape[1]),
        count, flat_order, flat_blocks, codes, local_dec,
        2 * pairs * TILE * BLOCK * local_dec.shape[1], pairs * BLOCK * local_dec.shape[1] * 2,
    )
    rebuilt = lax.psum_scatter(partial, "latent", scatter_dimension=0, tiled=True)
    return (rebuilt + dec_bias).astype(jnp.bfloat16)[None]


def solution(mesh):
    placed = (
        P("section", "latent", "tok"),
        P("section", "tok", "latent"),
        P("latent"),
        P("latent", "section", "tok"),
        P("section", "tok"),
        P(),
        P(),
    )
    return jax.shard_map(
        shards, mesh=mesh, in_specs=placed, out_specs=P("section", "latent", "tok"), check_vma=False
    )
```

```python
import functools

import jax
import jax.numpy as jnp
from jax import lax
from jax.experimental import pallas as pl
from jax.experimental.pallas import tpu as pltpu
from jax.sharding import PartitionSpec as P

BLOCK = 128
TILE = 128


def slot_table(active_blocks, block_counts, first_block, blocks_local, slots):
    listed = active_blocks.shape[1]
    slot_ids = jnp.arange(listed, dtype=jnp.int32)
    local = active_blocks - first_block
    valid = (slot_ids[None, :] < block_counts[:, None]) & (local >= 0) & (local < blocks_local)
    order = jnp.argsort(jnp.logical_not(valid).astype(jnp.int32), axis=1, stable=True)[:, :slots]
    picked_valid = jnp.take_along_axis(valid, order, axis=1)
    picked = jnp.where(picked_valid, jnp.take_along_axis(local, order, axis=1), 0)
    flat_valid = picked_valid.reshape(-1)
    flat_order = jnp.argsort(jnp.logical_not(flat_valid).astype(jnp.int32), stable=True).astype(jnp.int32)
    flat_blocks = picked.reshape(-1)[flat_order]
    count = jnp.sum(flat_valid.astype(jnp.int32)).reshape(1)
    return picked_valid, count, flat_order, flat_blocks


DEPTH = 6


def weight_stream(n, blk_ref, source, buf, sem, compute):
    def copy(i, slot):
        return pltpu.make_async_copy(source(blk_ref[i]), buf.at[slot], sem.at[slot])

    for j in range(DEPTH):
        @pl.when(j < n)
        def _():
            copy(j, j).start()

    def body(i, carry):
        slot = i % DEPTH
        copy(i, slot).wait()
        compute(i, buf.at[slot])

        @pl.when(i + DEPTH < n)
        def _():
            copy(i + DEPTH, slot).start()

        return carry

    lax.fori_loop(0, n, body, 0)


def encode_kernel(n_ref, slot_ref, blk_ref, acts_ref, enc_hbm, out_ref, buf, sem):
    slots = out_ref.shape[1]
    out_ref[...] = jnp.zeros(out_ref.shape, out_ref.dtype)

    def source(b):
        return enc_hbm.at[:, pl.ds(pl.multiple_of(b * BLOCK, BLOCK), BLOCK)]

    def compute(i, block):
        s = slot_ref[i]
        t = s // slots
        k = s % slots
        rows = acts_ref[pl.ds(pl.multiple_of(t * TILE, TILE), TILE), :]
        out_ref[t, k] = jnp.dot(rows, block[...], preferred_element_type=jnp.float32)

    weight_stream(n_ref[0], blk_ref, source, buf, sem, compute)


def decode_kernel(n_ref, slot_ref, blk_ref, codes_ref, dec_hbm, out_ref, buf, sem):
    slots = codes_ref.shape[1]
    out_ref[...] = jnp.zeros(out_ref.shape, out_ref.dtype)

    def source(b):
        return dec_hbm.at[pl.ds(pl.multiple_of(b * BLOCK, BLOCK), BLOCK), :]

    def compute(i, block):
        s = slot_ref[i]
        t = s // slots
        k = s % slots
        rows = pl.ds(pl.multiple_of(t * TILE, TILE), TILE)
        out_ref[rows, :] += jnp.dot(codes_ref[t, k], block[...], preferred_element_type=jnp.float32)

    weight_stream(n_ref[0], blk_ref, source, buf, sem, compute)


def sparse_call(kernel, out_shape, buf_shape, count, flat_order, flat_blocks, dense, weight, flops, nbytes):
    smem = pl.BlockSpec(memory_space=pltpu.SMEM)
    return pl.pallas_call(
        kernel,
        out_shape=out_shape,
        in_specs=[smem, smem, smem, pl.BlockSpec(memory_space=pltpu.VMEM), pl.BlockSpec(memory_space=pl.ANY)],
        out_specs=pl.BlockSpec(memory_space=pltpu.VMEM),
        scratch_shapes=[pltpu.VMEM((DEPTH,) + buf_shape, weight.dtype), pltpu.SemaphoreType.DMA((DEPTH,))],
        cost_estimate=pl.CostEstimate(flops=flops, bytes_accessed=nbytes, transcendentals=0),
    )(count, flat_order, flat_blocks, dense, weight)


LINE_MAX = 4


def line_pairs(n, k, rightward):
    return [(i, i + k) if rightward else (i + k, i) for i in range(n - k)]


def line_gather(x, axis):
    n = lax.axis_size(axis)
    if n > LINE_MAX:
        return lax.all_gather(x, axis, axis=0, tiled=True)
    me = lax.axis_index(axis)
    parts = [x]
    sources = [me]
    for k in range(1, n):
        parts.append(lax.ppermute(x, axis, line_pairs(n, k, True)))
        sources.append(me - k)
        parts.append(lax.ppermute(x, axis, line_pairs(n, k, False)))
        sources.append(me + k)
    out = jnp.zeros((n,) + x.shape, x.dtype)
    for part, src in zip(parts, sources):
        ok = (src >= 0) & (src < n)
        out = lax.dynamic_update_index_in_dim(
            out, jnp.where(ok, part, out[jnp.clip(src, 0, n - 1)]), jnp.clip(src, 0, n - 1), 0
        )
    return out.reshape((n * x.shape[0],) + x.shape[1:])


def line_reduce_scatter(x, axis, wire):
    n = lax.axis_size(axis)
    if n > LINE_MAX:
        return lax.psum_scatter(x, axis, scatter_dimension=0, tiled=True)
    me = lax.axis_index(axis)
    chunks = x.reshape((n, x.shape[0] // n) + x.shape[1:])
    acc = lax.dynamic_index_in_dim(chunks, me, keepdims=False)
    for k in range(1, n):
        for rightward in (True, False):
            dest = jnp.clip(me + k if rightward else me - k, 0, n - 1)
            sent = lax.dynamic_index_in_dim(chunks, dest, keepdims=False).astype(wire)
            got = lax.ppermute(sent, axis, line_pairs(n, k, rightward))
            acc = acc + got.astype(x.dtype)
    return acc


def shards(acts, enc_weight, enc_bias, dec_weight, dec_bias, active_blocks, block_counts):
    local_enc = enc_weight[0]
    local_dec = dec_weight[:, 0, :]
    width, n_lat = local_enc.shape
    tokens_all = line_gather(acts[0], "latent")
    n_tok = tokens_all.shape[0]
    tiles = n_tok // TILE
    blocks_local = n_lat // BLOCK
    slots = min(active_blocks.shape[1], blocks_local)
    first_block = lax.axis_index("latent") * blocks_local
    picked_valid, count, flat_order, flat_blocks = slot_table(
        active_blocks, block_counts, first_block, blocks_local, slots
    )
    pairs = tiles * slots

    compact = sparse_call(
        encode_kernel,
        jax.ShapeDtypeStruct((tiles, slots, TILE, BLOCK), jnp.float32),
        (width, BLOCK),
        count, flat_order, flat_blocks, tokens_all, local_enc,
        2 * pairs * TILE * width * BLOCK, pairs * (width * BLOCK * 2 + TILE * BLOCK * 4),
    )
    shared = lax.psum_scatter(compact, ("section", "tok"), scatter_dimension=2, tiled=True)
    bias_slots = enc_bias.reshape(blocks_local, BLOCK)
    slot_blocks = jnp.zeros((tiles * slots,), jnp.int32).at[flat_order].set(flat_blocks).reshape(tiles, slots)
    bias_slots = bias_slots[slot_blocks]
    codes_part = jnp.where(
        picked_valid[:, :, None, None], jax.nn.relu(shared + bias_slots[:, :, None, :]), 0.0
    ).astype(jnp.bfloat16)
    codes = lax.all_gather(codes_part, ("section", "tok"), axis=2, tiled=True)

    partial = sparse_call(
        decode_kernel,
        jax.ShapeDtypeStruct((n_tok, local_dec.shape[1]), jnp.float32),
        (BLOCK, local_dec.shape[1]),
        count, flat_order, flat_blocks, codes, local_dec,
        2 * pairs * TILE * BLOCK * local_dec.shape[1], pairs * BLOCK * local_dec.shape[1] * 2,
    )
    rebuilt = line_reduce_scatter(partial, "latent", jnp.bfloat16)
    return (rebuilt + dec_bias).astype(jnp.bfloat16)[None]


def solution(mesh):
    placed = (
        P("section", "latent", "tok"),
        P("section", "tok", "latent"),
        P("latent"),
        P("latent", "section", "tok"),
        P("section", "tok"),
        P(),
        P(),
    )
    return jax.shard_map(
        shards, mesh=mesh, in_specs=placed, out_specs=P("section", "latent", "tok"), check_vma=False
    )
```

```python
import functools

import jax
import jax.numpy as jnp
from jax import lax
from jax.experimental import pallas as pl
from jax.experimental.pallas import tpu as pltpu
from jax.sharding import PartitionSpec as P

BLOCK = 128
TILE = 128


def slot_table(active_blocks, block_counts, first_block, blocks_local, slots):
    listed = active_blocks.shape[1]
    slot_ids = jnp.arange(listed, dtype=jnp.int32)
    local = active_blocks - first_block
    valid = (slot_ids[None, :] < block_counts[:, None]) & (local >= 0) & (local < blocks_local)
    order = jnp.argsort(jnp.logical_not(valid).astype(jnp.int32), axis=1, stable=True)[:, :slots]
    picked_valid = jnp.take_along_axis(valid, order, axis=1)
    picked = jnp.where(picked_valid, jnp.take_along_axis(local, order, axis=1), 0)
    flat_valid = picked_valid.reshape(-1)
    flat_order = jnp.argsort(jnp.logical_not(flat_valid).astype(jnp.int32), stable=True).astype(jnp.int32)
    flat_blocks = picked.reshape(-1)[flat_order]
    count = jnp.sum(flat_valid.astype(jnp.int32)).reshape(1)
    return picked_valid, count, flat_order, flat_blocks


DEPTH = 6


def weight_stream(n, blk_ref, source, buf, sem, compute):
    def copy(i, slot):
        return pltpu.make_async_copy(source(blk_ref[i]), buf.at[slot], sem.at[slot])

    for j in range(DEPTH):
        @pl.when(j < n)
        def _():
            copy(j, j).start()

    def body(i, carry):
        slot = i % DEPTH
        copy(i, slot).wait()
        compute(i, buf.at[slot])

        @pl.when(i + DEPTH < n)
        def _():
            copy(i + DEPTH, slot).start()

        return carry

    lax.fori_loop(0, n, body, 0)


def encode_kernel(n_ref, slot_ref, blk_ref, acts_ref, enc_hbm, out_ref, buf, sem):
    slots = out_ref.shape[1]
    out_ref[...] = jnp.zeros(out_ref.shape, out_ref.dtype)

    def source(b):
        return enc_hbm.at[:, pl.ds(pl.multiple_of(b * BLOCK, BLOCK), BLOCK)]

    def compute(i, block):
        s = slot_ref[i]
        t = s // slots
        k = s % slots
        rows = acts_ref[pl.ds(pl.multiple_of(t * TILE, TILE), TILE), :]
        out_ref[t, k] = jnp.dot(rows, block[...], preferred_element_type=jnp.float32)

    weight_stream(n_ref[0], blk_ref, source, buf, sem, compute)


def decode_kernel(n_ref, slot_ref, blk_ref, codes_ref, dec_hbm, out_ref, buf, sem):
    slots = codes_ref.shape[1]
    out_ref[...] = jnp.zeros(out_ref.shape, out_ref.dtype)

    def source(b):
        return dec_hbm.at[pl.ds(pl.multiple_of(b * BLOCK, BLOCK), BLOCK), :]

    def compute(i, block):
        s = slot_ref[i]
        t = s // slots
        k = s % slots
        rows = pl.ds(pl.multiple_of(t * TILE, TILE), TILE)
        out_ref[rows, :] += jnp.dot(codes_ref[t, k], block[...], preferred_element_type=jnp.float32)

    weight_stream(n_ref[0], blk_ref, source, buf, sem, compute)


def sparse_call(kernel, out_shape, buf_shape, count, flat_order, flat_blocks, dense, weight, flops, nbytes):
    smem = pl.BlockSpec(memory_space=pltpu.SMEM)
    return pl.pallas_call(
        kernel,
        out_shape=out_shape,
        in_specs=[smem, smem, smem, pl.BlockSpec(memory_space=pltpu.VMEM), pl.BlockSpec(memory_space=pl.ANY)],
        out_specs=pl.BlockSpec(memory_space=pltpu.VMEM),
        scratch_shapes=[pltpu.VMEM((DEPTH,) + buf_shape, weight.dtype), pltpu.SemaphoreType.DMA((DEPTH,))],
        cost_estimate=pl.CostEstimate(flops=flops, bytes_accessed=nbytes, transcendentals=0),
    )(count, flat_order, flat_blocks, dense, weight)


LINE_MAX = 4
FEW = 16


def line_pairs(n, k, rightward):
    return [(i, i + k) if rightward else (i + k, i) for i in range(n - k)]


def line_gather(x, axis):
    n = lax.axis_size(axis)
    if n > LINE_MAX:
        return lax.all_gather(x, axis, axis=0, tiled=True)
    me = lax.axis_index(axis)
    parts = [x]
    sources = [me]
    for k in range(1, n):
        parts.append(lax.ppermute(x, axis, line_pairs(n, k, True)))
        sources.append(me - k)
        parts.append(lax.ppermute(x, axis, line_pairs(n, k, False)))
        sources.append(me + k)
    out = jnp.zeros((n,) + x.shape, x.dtype)
    for part, src in zip(parts, sources):
        ok = (src >= 0) & (src < n)
        out = lax.dynamic_update_index_in_dim(
            out, jnp.where(ok, part, out[jnp.clip(src, 0, n - 1)]), jnp.clip(src, 0, n - 1), 0
        )
    return out.reshape((n * x.shape[0],) + x.shape[1:])


def line_reduce_scatter(x, axis, wire):
    n = lax.axis_size(axis)
    if n > LINE_MAX:
        return lax.psum_scatter(x, axis, scatter_dimension=0, tiled=True)
    me = lax.axis_index(axis)
    chunks = x.reshape((n, x.shape[0] // n) + x.shape[1:])
    acc = lax.dynamic_index_in_dim(chunks, me, keepdims=False)
    for k in range(1, n):
        for rightward in (True, False):
            dest = jnp.clip(me + k if rightward else me - k, 0, n - 1)
            sent = lax.dynamic_index_in_dim(chunks, dest, keepdims=False).astype(wire)
            got = lax.ppermute(sent, axis, line_pairs(n, k, rightward))
            acc = acc + got.astype(x.dtype)
    return acc


def shards(acts, enc_weight, enc_bias, dec_weight, dec_bias, active_blocks, block_counts):
    local_enc = enc_weight[0]
    local_dec = dec_weight[:, 0, :]
    width, n_lat = local_enc.shape
    tokens_all = line_gather(acts[0], "latent")
    n_tok = tokens_all.shape[0]
    tiles = n_tok // TILE
    blocks_local = n_lat // BLOCK
    most = min(active_blocks.shape[1], blocks_local)
    first_block = lax.axis_index("latent") * blocks_local

    def middle(slots):
        picked_valid, count, flat_order, flat_blocks = slot_table(
            active_blocks, block_counts, first_block, blocks_local, slots
        )
        pairs = tiles * slots
        compact = sparse_call(
            encode_kernel,
            jax.ShapeDtypeStruct((tiles, slots, TILE, BLOCK), jnp.float32),
            (width, BLOCK),
            count, flat_order, flat_blocks, tokens_all, local_enc,
            2 * pairs * TILE * width * BLOCK, pairs * (width * BLOCK * 2 + TILE * BLOCK * 4),
        )
        shared = lax.psum_scatter(compact, ("section", "tok"), scatter_dimension=2, tiled=True)
        slot_blocks = jnp.zeros((pairs,), jnp.int32).at[flat_order].set(flat_blocks).reshape(tiles, slots)
        bias_slots = enc_bias.reshape(blocks_local, BLOCK)[slot_blocks]
        codes_part = jnp.where(
            picked_valid[:, :, None, None], jax.nn.relu(shared + bias_slots[:, :, None, :]), 0.0
        ).astype(jnp.bfloat16)
        codes = lax.all_gather(codes_part, ("section", "tok"), axis=2, tiled=True)
        return sparse_call(
            decode_kernel,
            jax.ShapeDtypeStruct((n_tok, local_dec.shape[1]), jnp.float32),
            (BLOCK, local_dec.shape[1]),
            count, flat_order, flat_blocks, codes, local_dec,
            2 * pairs * TILE * BLOCK * local_dec.shape[1], pairs * BLOCK * local_dec.shape[1] * 2,
        )

    if most > FEW:
        listed = jnp.arange(active_blocks.shape[1], dtype=jnp.int32)[None, :] < block_counts[:, None]
        shard_of = active_blocks // blocks_local
        per_shard = jnp.stack(
            [jnp.sum((listed & (shard_of == s)).astype(jnp.int32), axis=1) for s in range(lax.axis_size("latent"))]
        )
        branch = (jnp.max(per_shard) > FEW).astype(jnp.int32)
        partial = lax.switch(branch, [lambda: middle(FEW), lambda: middle(most)])
    else:
        partial = middle(most)
    rebuilt = line_reduce_scatter(partial, "latent", jnp.bfloat16)
    return (rebuilt + dec_bias).astype(jnp.bfloat16)[None]


def solution(mesh):
    placed = (
        P("section", "latent", "tok"),
        P("section", "tok", "latent"),
        P("latent"),
        P("latent", "section", "tok"),
        P("section", "tok"),
        P(),
        P(),
    )
    return jax.shard_map(
        shards, mesh=mesh, in_specs=placed, out_specs=P("section", "latent", "tok"), check_vma=False
    )
```

```python
import functools

import jax
import jax.numpy as jnp
from jax import lax
from jax.experimental import pallas as pl
from jax.experimental.pallas import tpu as pltpu
from jax.sharding import PartitionSpec as P

BLOCK = 128
TILE = 128


def slot_table(active_blocks, block_counts, first_block, blocks_local, slots):
    listed = active_blocks.shape[1]
    slot_ids = jnp.arange(listed, dtype=jnp.int32)
    local = active_blocks - first_block
    valid = (slot_ids[None, :] < block_counts[:, None]) & (local >= 0) & (local < blocks_local)
    order = jnp.argsort(jnp.logical_not(valid).astype(jnp.int32), axis=1, stable=True)[:, :slots]
    picked_valid = jnp.take_along_axis(valid, order, axis=1)
    picked = jnp.where(picked_valid, jnp.take_along_axis(local, order, axis=1), 0)
    flat_valid = picked_valid.reshape(-1)
    flat_order = jnp.argsort(jnp.logical_not(flat_valid).astype(jnp.int32), stable=True).astype(jnp.int32)
    flat_blocks = picked.reshape(-1)[flat_order]
    count = jnp.sum(flat_valid.astype(jnp.int32)).reshape(1)
    return picked_valid, count, flat_order, flat_blocks


DEPTH = 6


def weight_stream(n, blk_ref, source, buf, sem, compute):
    def copy(i, slot):
        return pltpu.make_async_copy(source(blk_ref[i]), buf.at[slot], sem.at[slot])

    for j in range(DEPTH):
        @pl.when(j < n)
        def _():
            copy(j, j).start()

    def body(i, carry):
        slot = i % DEPTH
        copy(i, slot).wait()
        compute(i, buf.at[slot])

        @pl.when(i + DEPTH < n)
        def _():
            copy(i + DEPTH, slot).start()

        return carry

    lax.fori_loop(0, n, body, 0)


def encode_kernel(n_ref, slot_ref, blk_ref, acts_ref, enc_hbm, out_ref, buf, sem):
    slots = out_ref.shape[1]
    out_ref[...] = jnp.zeros(out_ref.shape, out_ref.dtype)

    def source(b):
        return enc_hbm.at[:, pl.ds(pl.multiple_of(b * BLOCK, BLOCK), BLOCK)]

    def compute(i, block):
        s = slot_ref[i]
        t = s // slots
        k = s % slots
        rows = acts_ref[pl.ds(pl.multiple_of(t * TILE, TILE), TILE), :]
        out_ref[t, k] = jnp.dot(rows, block[...], preferred_element_type=jnp.float32)

    weight_stream(n_ref[0], blk_ref, source, buf, sem, compute)


def decode_kernel(n_ref, slot_ref, blk_ref, codes_ref, dec_hbm, out_ref, buf, sem):
    slots = codes_ref.shape[1]
    out_ref[...] = jnp.zeros(out_ref.shape, out_ref.dtype)

    def source(b):
        return dec_hbm.at[pl.ds(pl.multiple_of(b * BLOCK, BLOCK), BLOCK), :]

    def compute(i, block):
        s = slot_ref[i]
        t = s // slots
        k = s % slots
        rows = pl.ds(pl.multiple_of(t * TILE, TILE), TILE)
        out_ref[rows, :] += jnp.dot(codes_ref[t, k], block[...], preferred_element_type=jnp.float32)

    weight_stream(n_ref[0], blk_ref, source, buf, sem, compute)


def sparse_call(kernel, out_shape, buf_shape, count, flat_order, flat_blocks, dense, weight, flops, nbytes):
    smem = pl.BlockSpec(memory_space=pltpu.SMEM)
    return pl.pallas_call(
        kernel,
        out_shape=out_shape,
        in_specs=[smem, smem, smem, pl.BlockSpec(memory_space=pltpu.VMEM), pl.BlockSpec(memory_space=pl.ANY)],
        out_specs=pl.BlockSpec(memory_space=pltpu.VMEM),
        scratch_shapes=[pltpu.VMEM((DEPTH,) + buf_shape, weight.dtype), pltpu.SemaphoreType.DMA((DEPTH,))],
        cost_estimate=pl.CostEstimate(flops=flops, bytes_accessed=nbytes, transcendentals=0),
    )(count, flat_order, flat_blocks, dense, weight)


LINE_MAX = 4
FEW = 16


def line_pairs(n, k, rightward):
    return [(i, i + k) if rightward else (i + k, i) for i in range(n - k)]


def line_gather(x, axis):
    n = lax.axis_size(axis)
    if n > LINE_MAX:
        return lax.all_gather(x, axis, axis=0, tiled=True)
    me = lax.axis_index(axis)
    parts = [x]
    sources = [me]
    for k in range(1, n):
        parts.append(lax.ppermute(x, axis, line_pairs(n, k, True)))
        sources.append(me - k)
        parts.append(lax.ppermute(x, axis, line_pairs(n, k, False)))
        sources.append(me + k)
    out = jnp.zeros((n,) + x.shape, x.dtype)
    for part, src in zip(parts, sources):
        ok = (src >= 0) & (src < n)
        out = lax.dynamic_update_index_in_dim(
            out, jnp.where(ok, part, out[jnp.clip(src, 0, n - 1)]), jnp.clip(src, 0, n - 1), 0
        )
    return out.reshape((n * x.shape[0],) + x.shape[1:])


def line_reduce_scatter(x, axis, wire):
    n = lax.axis_size(axis)
    if n > LINE_MAX:
        return lax.psum_scatter(x, axis, scatter_dimension=0, tiled=True)
    me = lax.axis_index(axis)
    chunks = x.reshape((n, x.shape[0] // n) + x.shape[1:])
    acc = lax.dynamic_index_in_dim(chunks, me, keepdims=False)
    for k in range(1, n):
        for rightward in (True, False):
            dest = jnp.clip(me + k if rightward else me - k, 0, n - 1)
            sent = lax.dynamic_index_in_dim(chunks, dest, keepdims=False).astype(wire)
            got = lax.ppermute(sent, axis, line_pairs(n, k, rightward))
            acc = acc + got.astype(x.dtype)
    return acc


def halving_steps():
    steps = []
    for axis in ("section", "tok"):
        n = lax.axis_size(axis)
        if n & (n - 1):
            return None
        me = lax.axis_index(axis)
        level = n // 2
        while level:
            steps.append((axis, (me // level) % 2, [(i, i ^ level) for i in range(n)]))
            level //= 2
    return steps


def halving_sum(x, steps):
    for axis, bit, perm in steps:
        half = x.shape[2] // 2
        keep = lax.dynamic_slice_in_dim(x, bit * half, half, axis=2)
        send = lax.dynamic_slice_in_dim(x, (1 - bit) * half, half, axis=2)
        x = keep + lax.ppermute(send, axis, perm)
    return x


def doubling_gather(x, steps):
    for axis, bit, perm in reversed(steps):
        got = lax.ppermute(x, axis, perm)
        x = jnp.where(bit == 0, jnp.concatenate([x, got], axis=2), jnp.concatenate([got, x], axis=2))
    return x


def shards(acts, enc_weight, enc_bias, dec_weight, dec_bias, active_blocks, block_counts):
    local_enc = enc_weight[0]
    local_dec = dec_weight[:, 0, :]
    width, n_lat = local_enc.shape
    tokens_all = lax.all_gather(acts, "latent", axis=1, tiled=True)[0]
    n_tok = tokens_all.shape[0]
    tiles = n_tok // TILE
    blocks_local = n_lat // BLOCK
    most = min(active_blocks.shape[1], blocks_local)
    first_block = lax.axis_index("latent") * blocks_local

    def middle(slots):
        picked_valid, count, flat_order, flat_blocks = slot_table(
            active_blocks, block_counts, first_block, blocks_local, slots
        )
        pairs = tiles * slots
        compact = sparse_call(
            encode_kernel,
            jax.ShapeDtypeStruct((tiles, slots, TILE, BLOCK), jnp.float32),
            (width, BLOCK),
            count, flat_order, flat_blocks, tokens_all, local_enc,
            2 * pairs * TILE * width * BLOCK, pairs * (width * BLOCK * 2 + TILE * BLOCK * 4),
        )
        steps = halving_steps()
        if steps is None:
            shared = lax.psum_scatter(compact, ("section", "tok"), scatter_dimension=2, tiled=True)
        else:
            shared = halving_sum(compact, steps)
        slot_blocks = jnp.zeros((pairs,), jnp.int32).at[flat_order].set(flat_blocks).reshape(tiles, slots)
        bias_slots = enc_bias.reshape(blocks_local, BLOCK)[slot_blocks]
        codes_part = jnp.where(
            picked_valid[:, :, None, None], jax.nn.relu(shared + bias_slots[:, :, None, :]), 0.0
        ).astype(jnp.bfloat16)
        if steps is None:
            codes = lax.all_gather(codes_part, ("section", "tok"), axis=2, tiled=True)
        else:
            codes = doubling_gather(codes_part, steps)
        return sparse_call(
            decode_kernel,
            jax.ShapeDtypeStruct((n_tok, local_dec.shape[1]), jnp.float32),
            (BLOCK, local_dec.shape[1]),
            count, flat_order, flat_blocks, codes, local_dec,
            2 * pairs * TILE * BLOCK * local_dec.shape[1], pairs * BLOCK * local_dec.shape[1] * 2,
        )

    if most > FEW:
        listed = jnp.arange(active_blocks.shape[1], dtype=jnp.int32)[None, :] < block_counts[:, None]
        shard_of = active_blocks // blocks_local
        per_shard = jnp.stack(
            [jnp.sum((listed & (shard_of == s)).astype(jnp.int32), axis=1) for s in range(lax.axis_size("latent"))]
        )
        branch = (jnp.max(per_shard) > FEW).astype(jnp.int32)
        partial = lax.switch(branch, [lambda: middle(FEW), lambda: middle(most)])
    else:
        partial = middle(most)
    rebuilt = line_reduce_scatter(partial, "latent", jnp.bfloat16)
    return (rebuilt + dec_bias).astype(jnp.bfloat16)[None]


def solution(mesh):
    placed = (
        P("section", "latent", "tok"),
        P("section", "tok", "latent"),
        P("latent"),
        P("latent", "section", "tok"),
        P("section", "tok"),
        P(),
        P(),
    )
    return jax.shard_map(
        shards, mesh=mesh, in_specs=placed, out_specs=P("section", "latent", "tok"), check_vma=False
    )
```

```python
import functools

import jax
import jax.numpy as jnp
from jax import lax
from jax.experimental import pallas as pl
from jax.experimental.pallas import tpu as pltpu
from jax.sharding import PartitionSpec as P

BLOCK = 128
TILE = 128


def slot_table(active_blocks, block_counts, first_block, blocks_local, slots):
    listed = active_blocks.shape[1]
    slot_ids = jnp.arange(listed, dtype=jnp.int32)
    local = active_blocks - first_block
    valid = (slot_ids[None, :] < block_counts[:, None]) & (local >= 0) & (local < blocks_local)
    order = jnp.argsort(jnp.logical_not(valid).astype(jnp.int32), axis=1, stable=True)[:, :slots]
    picked_valid = jnp.take_along_axis(valid, order, axis=1)
    picked = jnp.where(picked_valid, jnp.take_along_axis(local, order, axis=1), 0)
    flat_valid = picked_valid.reshape(-1)
    flat_order = jnp.argsort(jnp.logical_not(flat_valid).astype(jnp.int32), stable=True).astype(jnp.int32)
    flat_blocks = picked.reshape(-1)[flat_order]
    count = jnp.sum(flat_valid.astype(jnp.int32)).reshape(1)
    return picked_valid, count, flat_order, flat_blocks


DEPTH = 6


def weight_stream(n, blk_ref, source, buf, sem, compute):
    def copy(i, slot):
        return pltpu.make_async_copy(source(blk_ref[i]), buf.at[slot], sem.at[slot])

    for j in range(DEPTH):
        @pl.when(j < n)
        def _():
            copy(j, j).start()

    def body(i, carry):
        slot = i % DEPTH
        copy(i, slot).wait()
        compute(i, buf.at[slot])

        @pl.when(i + DEPTH < n)
        def _():
            copy(i + DEPTH, slot).start()

        return carry

    lax.fori_loop(0, n, body, 0)


def encode_kernel(n_ref, slot_ref, blk_ref, acts_ref, enc_hbm, out_ref, buf, sem):
    slots = out_ref.shape[1]
    out_ref[...] = jnp.zeros(out_ref.shape, out_ref.dtype)

    def source(b):
        return enc_hbm.at[:, pl.ds(pl.multiple_of(b * BLOCK, BLOCK), BLOCK)]

    def compute(i, block):
        s = slot_ref[i]
        t = s // slots
        k = s % slots
        rows = acts_ref[pl.ds(pl.multiple_of(t * TILE, TILE), TILE), :]
        out_ref[t, k] = jnp.dot(rows, block[...], preferred_element_type=jnp.float32)

    weight_stream(n_ref[0], blk_ref, source, buf, sem, compute)


def decode_kernel(n_ref, slot_ref, blk_ref, codes_ref, dec_hbm, out_ref, buf, sem):
    slots = codes_ref.shape[1]
    out_ref[...] = jnp.zeros(out_ref.shape, out_ref.dtype)

    def source(b):
        return dec_hbm.at[pl.ds(pl.multiple_of(b * BLOCK, BLOCK), BLOCK), :]

    def compute(i, block):
        s = slot_ref[i]
        t = s // slots
        k = s % slots
        rows = pl.ds(pl.multiple_of(t * TILE, TILE), TILE)
        out_ref[rows, :] += jnp.dot(codes_ref[t, k], block[...], preferred_element_type=jnp.float32)

    weight_stream(n_ref[0], blk_ref, source, buf, sem, compute)


def sparse_call(kernel, out_shape, buf_shape, count, flat_order, flat_blocks, dense, weight, flops, nbytes):
    smem = pl.BlockSpec(memory_space=pltpu.SMEM)
    return pl.pallas_call(
        kernel,
        out_shape=out_shape,
        in_specs=[smem, smem, smem, pl.BlockSpec(memory_space=pltpu.VMEM), pl.BlockSpec(memory_space=pl.ANY)],
        out_specs=pl.BlockSpec(memory_space=pltpu.VMEM),
        scratch_shapes=[pltpu.VMEM((DEPTH,) + buf_shape, weight.dtype), pltpu.SemaphoreType.DMA((DEPTH,))],
        cost_estimate=pl.CostEstimate(flops=flops, bytes_accessed=nbytes, transcendentals=0),
    )(count, flat_order, flat_blocks, dense, weight)


LINE_MAX = 4
FEW = 16


def line_pairs(n, k, rightward):
    return [(i, i + k) if rightward else (i + k, i) for i in range(n - k)]


def line_gather(x, axis):
    n = lax.axis_size(axis)
    if n > LINE_MAX:
        return lax.all_gather(x, axis, axis=0, tiled=True)
    me = lax.axis_index(axis)
    parts = [x]
    sources = [me]
    for k in range(1, n):
        parts.append(lax.ppermute(x, axis, line_pairs(n, k, True)))
        sources.append(me - k)
        parts.append(lax.ppermute(x, axis, line_pairs(n, k, False)))
        sources.append(me + k)
    out = jnp.zeros((n,) + x.shape, x.dtype)
    for part, src in zip(parts, sources):
        ok = (src >= 0) & (src < n)
        out = lax.dynamic_update_index_in_dim(
            out, jnp.where(ok, part, out[jnp.clip(src, 0, n - 1)]), jnp.clip(src, 0, n - 1), 0
        )
    return out.reshape((n * x.shape[0],) + x.shape[1:])


def line_reduce_scatter(x, axis, wire):
    n = lax.axis_size(axis)
    if n > LINE_MAX or n & (n - 1):
        return lax.psum_scatter(x, axis, scatter_dimension=0, tiled=True)
    me = lax.axis_index(axis)
    rows = x.shape[0] // n
    bits = n.bit_length() - 1
    x = x.reshape((2,) * bits + (rows,) + x.shape[1:])
    for j in range(bits):
        level = 1 << j
        bit = (me // level) % 2
        keep = lax.dynamic_index_in_dim(x, bit, axis=bits - 1 - j, keepdims=False)
        send = lax.dynamic_index_in_dim(x, 1 - bit, axis=bits - 1 - j, keepdims=False).astype(wire)
        x = keep + lax.ppermute(send, axis, [(i, i ^ level) for i in range(n)]).astype(keep.dtype)
    return x


def halving_steps():
    steps = []
    for axis in ("section", "tok"):
        n = lax.axis_size(axis)
        if n & (n - 1):
            return None
        me = lax.axis_index(axis)
        level = n // 2
        while level:
            steps.append((axis, (me // level) % 2, [(i, i ^ level) for i in range(n)]))
            level //= 2
    return steps


def halving_sum(x, steps):
    for axis, bit, perm in steps:
        half = x.shape[2] // 2
        keep = lax.dynamic_slice_in_dim(x, bit * half, half, axis=2)
        send = lax.dynamic_slice_in_dim(x, (1 - bit) * half, half, axis=2)
        x = keep + lax.ppermute(send, axis, perm)
    return x


def doubling_gather(x, steps):
    for axis, bit, perm in reversed(steps):
        got = lax.ppermute(x, axis, perm)
        x = jnp.where(bit == 0, jnp.concatenate([x, got], axis=2), jnp.concatenate([got, x], axis=2))
    return x


def shards(acts, enc_weight, enc_bias, dec_weight, dec_bias, active_blocks, block_counts):
    local_enc = enc_weight[0]
    local_dec = dec_weight[:, 0, :]
    width, n_lat = local_enc.shape
    tokens_all = lax.all_gather(acts, "latent", axis=1, tiled=True)[0]
    n_tok = tokens_all.shape[0]
    tiles = n_tok // TILE
    blocks_local = n_lat // BLOCK
    most = min(active_blocks.shape[1], blocks_local)
    first_block = lax.axis_index("latent") * blocks_local

    def middle(slots, table):
        picked_valid, count, flat_order, flat_blocks = table
        pairs = tiles * slots
        compact = sparse_call(
            encode_kernel,
            jax.ShapeDtypeStruct((tiles, slots, TILE, BLOCK), jnp.float32),
            (width, BLOCK),
            count, flat_order, flat_blocks, tokens_all, local_enc,
            2 * pairs * TILE * width * BLOCK, pairs * (width * BLOCK * 2 + TILE * BLOCK * 4),
        )
        steps = halving_steps()
        if steps is None:
            shared = lax.psum_scatter(compact, ("section", "tok"), scatter_dimension=2, tiled=True)
        else:
            shared = halving_sum(compact, steps)
        slot_blocks = jnp.zeros((pairs,), jnp.int32).at[flat_order].set(flat_blocks).reshape(tiles, slots)
        bias_slots = enc_bias.reshape(blocks_local, BLOCK)[slot_blocks]
        codes_part = jnp.where(
            picked_valid[:, :, None, None], jax.nn.relu(shared + bias_slots[:, :, None, :]), 0.0
        ).astype(jnp.bfloat16)
        if steps is None:
            codes = lax.all_gather(codes_part, ("section", "tok"), axis=2, tiled=True)
        else:
            codes = doubling_gather(codes_part, steps)
        return sparse_call(
            decode_kernel,
            jax.ShapeDtypeStruct((n_tok, local_dec.shape[1]), jnp.float32),
            (BLOCK, local_dec.shape[1]),
            count, flat_order, flat_blocks, codes, local_dec,
            2 * pairs * TILE * BLOCK * local_dec.shape[1], pairs * BLOCK * local_dec.shape[1] * 2,
        )

    if most > FEW:
        listed = jnp.arange(active_blocks.shape[1], dtype=jnp.int32)[None, :] < block_counts[:, None]
        shard_of = active_blocks // blocks_local
        per_shard = jnp.stack(
            [jnp.sum((listed & (shard_of == s)).astype(jnp.int32), axis=1) for s in range(lax.axis_size("latent"))]
        )
        branch = (jnp.max(per_shard) > FEW).astype(jnp.int32)
        few_table = slot_table(active_blocks, block_counts, first_block, blocks_local, FEW)
        most_table = slot_table(active_blocks, block_counts, first_block, blocks_local, most)
        partial = lax.switch(branch, [lambda: middle(FEW, few_table), lambda: middle(most, most_table)])
    else:
        partial = middle(most, slot_table(active_blocks, block_counts, first_block, blocks_local, most))
    rebuilt = line_reduce_scatter(partial, "latent", jnp.bfloat16)
    return (rebuilt + dec_bias).astype(jnp.bfloat16)[None]


def solution(mesh):
    placed = (
        P("section", "latent", "tok"),
        P("section", "tok", "latent"),
        P("latent"),
        P("latent", "section", "tok"),
        P("section", "tok"),
        P(),
        P(),
    )
    return jax.shard_map(
        shards, mesh=mesh, in_specs=placed, out_specs=P("section", "latent", "tok"), check_vma=False
    )
```

```python
import functools

import jax
import jax.numpy as jnp
from jax import lax
from jax.experimental import pallas as pl
from jax.experimental.pallas import tpu as pltpu
from jax.sharding import PartitionSpec as P

BLOCK = 128
TILE = 128


def pair_table(active_blocks, block_counts, first_block, blocks_local, capacity):
    tiles, listed = active_blocks.shape
    slot_ids = jnp.arange(listed, dtype=jnp.int32)
    local = active_blocks - first_block
    valid = ((slot_ids[None, :] < block_counts[:, None]) & (local >= 0) & (local < blocks_local)).reshape(-1)
    order = jnp.argsort(jnp.logical_not(valid).astype(jnp.int32), stable=True)[:capacity].astype(jnp.int32)
    pair_valid = valid[order]
    pair_tile = order // listed
    pair_block = jnp.where(pair_valid, local.reshape(-1)[order], 0)
    count = jnp.minimum(jnp.sum(valid.astype(jnp.int32)), capacity).reshape(1)
    return pair_valid, count, pair_tile, pair_block


DEPTH = 6


def weight_stream(n, blk_ref, source, buf, sem, compute):
    def copy(i, slot):
        return pltpu.make_async_copy(source(blk_ref[i]), buf.at[slot], sem.at[slot])

    for j in range(DEPTH):
        @pl.when(j < n)
        def _():
            copy(j, j).start()

    def body(i, carry):
        slot = i % DEPTH
        copy(i, slot).wait()
        compute(i, buf.at[slot])

        @pl.when(i + DEPTH < n)
        def _():
            copy(i + DEPTH, slot).start()

        return carry

    lax.fori_loop(0, n, body, 0)


def encode_kernel(n_ref, tile_ref, blk_ref, acts_ref, enc_hbm, out_ref, buf, sem):
    out_ref[...] = jnp.zeros(out_ref.shape, out_ref.dtype)

    def source(b):
        return enc_hbm.at[:, pl.ds(pl.multiple_of(b * BLOCK, BLOCK), BLOCK)]

    def compute(i, block):
        rows = acts_ref[pl.ds(pl.multiple_of(tile_ref[i] * TILE, TILE), TILE), :]
        out_ref[i] = jnp.dot(rows, block[...], preferred_element_type=jnp.float32)

    weight_stream(n_ref[0], blk_ref, source, buf, sem, compute)


def decode_kernel(n_ref, tile_ref, blk_ref, codes_ref, dec_hbm, out_ref, buf, sem):
    out_ref[...] = jnp.zeros(out_ref.shape, out_ref.dtype)

    def source(b):
        return dec_hbm.at[pl.ds(pl.multiple_of(b * BLOCK, BLOCK), BLOCK), :]

    def compute(i, block):
        rows = pl.ds(pl.multiple_of(tile_ref[i] * TILE, TILE), TILE)
        out_ref[rows, :] += jnp.dot(codes_ref[i], block[...], preferred_element_type=jnp.float32)

    weight_stream(n_ref[0], blk_ref, source, buf, sem, compute)


def sparse_call(kernel, out_shape, buf_shape, count, pair_tile, pair_block, dense, weight, flops, nbytes):
    smem = pl.BlockSpec(memory_space=pltpu.SMEM)
    return pl.pallas_call(
        kernel,
        out_shape=out_shape,
        in_specs=[smem, smem, smem, pl.BlockSpec(memory_space=pltpu.VMEM), pl.BlockSpec(memory_space=pl.ANY)],
        out_specs=pl.BlockSpec(memory_space=pltpu.VMEM),
        scratch_shapes=[pltpu.VMEM((DEPTH,) + buf_shape, weight.dtype), pltpu.SemaphoreType.DMA((DEPTH,))],
        cost_estimate=pl.CostEstimate(flops=flops, bytes_accessed=nbytes, transcendentals=0),
    )(count, pair_tile, pair_block, dense, weight)


LINE_MAX = 4
CAPACITIES = (16, 24)


def line_pairs(n, k, rightward):
    return [(i, i + k) if rightward else (i + k, i) for i in range(n - k)]


def line_gather(x, axis):
    n = lax.axis_size(axis)
    if n > LINE_MAX:
        return lax.all_gather(x, axis, axis=0, tiled=True)
    me = lax.axis_index(axis)
    parts = [x]
    sources = [me]
    for k in range(1, n):
        parts.append(lax.ppermute(x, axis, line_pairs(n, k, True)))
        sources.append(me - k)
        parts.append(lax.ppermute(x, axis, line_pairs(n, k, False)))
        sources.append(me + k)
    out = jnp.zeros((n,) + x.shape, x.dtype)
    for part, src in zip(parts, sources):
        ok = (src >= 0) & (src < n)
        out = lax.dynamic_update_index_in_dim(
            out, jnp.where(ok, part, out[jnp.clip(src, 0, n - 1)]), jnp.clip(src, 0, n - 1), 0
        )
    return out.reshape((n * x.shape[0],) + x.shape[1:])


def line_reduce_scatter(x, axis, wire):
    n = lax.axis_size(axis)
    if n > LINE_MAX or n & (n - 1):
        return lax.psum_scatter(x, axis, scatter_dimension=0, tiled=True)
    me = lax.axis_index(axis)
    rows = x.shape[0] // n
    bits = n.bit_length() - 1
    x = x.reshape((2,) * bits + (rows,) + x.shape[1:])
    for j in range(bits):
        level = 1 << j
        bit = (me // level) % 2
        keep = lax.dynamic_index_in_dim(x, bit, axis=bits - 1 - j, keepdims=False)
        send = lax.dynamic_index_in_dim(x, 1 - bit, axis=bits - 1 - j, keepdims=False).astype(wire)
        x = keep + lax.ppermute(send, axis, [(i, i ^ level) for i in range(n)]).astype(keep.dtype)
    return x


def halving_steps():
    steps = []
    for axis in ("section", "tok"):
        n = lax.axis_size(axis)
        if n & (n - 1):
            return None
        me = lax.axis_index(axis)
        level = n // 2
        while level:
            steps.append((axis, (me // level) % 2, [(i, i ^ level) for i in range(n)]))
            level //= 2
    return steps


def halving_sum(x, steps):
    for axis, bit, perm in steps:
        half = x.shape[1] // 2
        keep = lax.dynamic_slice_in_dim(x, bit * half, half, axis=1)
        send = lax.dynamic_slice_in_dim(x, (1 - bit) * half, half, axis=1)
        x = keep + lax.ppermute(send, axis, perm)
    return x


def doubling_gather(x, steps):
    for axis, bit, perm in reversed(steps):
        got = lax.ppermute(x, axis, perm)
        x = jnp.where(bit == 0, jnp.concatenate([x, got], axis=1), jnp.concatenate([got, x], axis=1))
    return x


def shards(acts, enc_weight, enc_bias, dec_weight, dec_bias, active_blocks, block_counts):
    local_enc = enc_weight[0]
    local_dec = dec_weight[:, 0, :]
    width, n_lat = local_enc.shape
    tokens_all = lax.all_gather(acts, "latent", axis=1, tiled=True)[0]
    n_tok = tokens_all.shape[0]
    tiles = n_tok // TILE
    blocks_local = n_lat // BLOCK
    most = tiles * min(active_blocks.shape[1], blocks_local)
    first_block = lax.axis_index("latent") * blocks_local

    def table(capacity):
        return pair_table(active_blocks, block_counts, first_block, blocks_local, capacity)

    def middle(capacity, pairs):
        pair_valid, count, pair_tile, pair_block = pairs
        compact = sparse_call(
            encode_kernel,
            jax.ShapeDtypeStruct((capacity, TILE, BLOCK), jnp.float32),
            (width, BLOCK),
            count, pair_tile, pair_block, tokens_all, local_enc,
            2 * capacity * TILE * width * BLOCK, capacity * (width * BLOCK * 2 + TILE * BLOCK * 4),
        )
        steps = halving_steps()
        if steps is None:
            shared = lax.psum_scatter(compact, ("section", "tok"), scatter_dimension=1, tiled=True)
        else:
            shared = halving_sum(compact, steps)
        bias_pairs = enc_bias.reshape(blocks_local, BLOCK)[pair_block]
        codes_part = jnp.where(
            pair_valid[:, None, None], jax.nn.relu(shared + bias_pairs[:, None, :]), 0.0
        ).astype(jnp.bfloat16)
        if steps is None:
            codes = lax.all_gather(codes_part, ("section", "tok"), axis=1, tiled=True)
        else:
            codes = doubling_gather(codes_part, steps)
        return sparse_call(
            decode_kernel,
            jax.ShapeDtypeStruct((n_tok, local_dec.shape[1]), jnp.float32),
            (BLOCK, local_dec.shape[1]),
            count, pair_tile, pair_block, codes, local_dec,
            2 * capacity * TILE * BLOCK * local_dec.shape[1], capacity * BLOCK * local_dec.shape[1] * 2,
        )

    levels = [c for c in CAPACITIES if c < most]
    if levels:
        listed = jnp.arange(active_blocks.shape[1], dtype=jnp.int32)[None, :] < block_counts[:, None]
        shard_of = active_blocks // blocks_local
        fullest = jnp.max(
            jnp.stack([jnp.sum((listed & (shard_of == s)).astype(jnp.int32)) for s in range(lax.axis_size("latent"))])
        )
        branch = sum((fullest > c).astype(jnp.int32) for c in levels)
        tables = [table(c) for c in levels + [most]]
        partial = lax.switch(branch, [functools.partial(middle, c, t) for c, t in zip(levels + [most], tables)])
    else:
        partial = middle(most, table(most))
    rebuilt = line_reduce_scatter(partial, "latent", jnp.bfloat16)
    return (rebuilt + dec_bias).astype(jnp.bfloat16)[None]


def solution(mesh):
    placed = (
        P("section", "latent", "tok"),
        P("section", "tok", "latent"),
        P("latent"),
        P("latent", "section", "tok"),
        P("section", "tok"),
        P(),
        P(),
    )
    return jax.shard_map(
        shards, mesh=mesh, in_specs=placed, out_specs=P("section", "latent", "tok"), check_vma=False
    )
```

```python
import functools

import jax
import jax.numpy as jnp
from jax import lax
from jax.experimental import pallas as pl
from jax.experimental.pallas import tpu as pltpu
from jax.sharding import PartitionSpec as P

BLOCK = 128
TILE = 128


def pair_table(active_blocks, block_counts, first_block, blocks_local, capacity):
    tiles, listed = active_blocks.shape
    slot_ids = jnp.arange(listed, dtype=jnp.int32)
    local = active_blocks - first_block
    valid = ((slot_ids[None, :] < block_counts[:, None]) & (local >= 0) & (local < blocks_local)).reshape(-1)
    order = jnp.argsort(jnp.logical_not(valid).astype(jnp.int32), stable=True)[:capacity].astype(jnp.int32)
    pair_valid = valid[order]
    pair_tile = order // listed
    pair_block = jnp.where(pair_valid, local.reshape(-1)[order], 0)
    count = jnp.minimum(jnp.sum(valid.astype(jnp.int32)), capacity).reshape(1)
    return pair_valid, count, pair_tile, pair_block


DEPTH = 6


def weight_stream(n, blk_ref, source, buf, sem, compute):
    def copy(i, slot):
        return pltpu.make_async_copy(source(blk_ref[i]), buf.at[slot], sem.at[slot])

    for j in range(DEPTH):
        @pl.when(j < n)
        def _():
            copy(j, j).start()

    def body(i, carry):
        slot = i % DEPTH
        copy(i, slot).wait()
        compute(i, buf.at[slot])

        @pl.when(i + DEPTH < n)
        def _():
            copy(i + DEPTH, slot).start()

        return carry

    lax.fori_loop(0, n, body, 0)


def encode_kernel(n_ref, tile_ref, blk_ref, acts_ref, enc_hbm, out_ref, buf, sem):
    out_ref[...] = jnp.zeros(out_ref.shape, out_ref.dtype)

    def source(b):
        return enc_hbm.at[:, pl.ds(pl.multiple_of(b * BLOCK, BLOCK), BLOCK)]

    def compute(i, block):
        rows = acts_ref[pl.ds(pl.multiple_of(tile_ref[i] * TILE, TILE), TILE), :]
        out_ref[i] = jnp.dot(rows, block[...], preferred_element_type=jnp.float32)

    weight_stream(n_ref[0], blk_ref, source, buf, sem, compute)


def decode_kernel(n_ref, tile_ref, blk_ref, codes_ref, dec_hbm, out_ref, buf, sem):
    out_ref[...] = jnp.zeros(out_ref.shape, out_ref.dtype)

    def source(b):
        return dec_hbm.at[pl.ds(pl.multiple_of(b * BLOCK, BLOCK), BLOCK), :]

    def compute(i, block):
        rows = pl.ds(pl.multiple_of(tile_ref[i] * TILE, TILE), TILE)
        out_ref[rows, :] += jnp.dot(codes_ref[i], block[...], preferred_element_type=jnp.float32)

    weight_stream(n_ref[0], blk_ref, source, buf, sem, compute)


def sparse_call(kernel, out_shape, buf_shape, count, pair_tile, pair_block, dense, weight, flops, nbytes):
    smem = pl.BlockSpec(memory_space=pltpu.SMEM)
    return pl.pallas_call(
        kernel,
        out_shape=out_shape,
        in_specs=[smem, smem, smem, pl.BlockSpec(memory_space=pltpu.VMEM), pl.BlockSpec(memory_space=pl.ANY)],
        out_specs=pl.BlockSpec(memory_space=pltpu.VMEM),
        scratch_shapes=[pltpu.VMEM((DEPTH,) + buf_shape, weight.dtype), pltpu.SemaphoreType.DMA((DEPTH,))],
        cost_estimate=pl.CostEstimate(flops=flops, bytes_accessed=nbytes, transcendentals=0),
    )(count, pair_tile, pair_block, dense, weight)


LINE_MAX = 4
CAPACITIES = (16, 24)
GATHERED = 16


def line_pairs(n, k, rightward):
    return [(i, i + k) if rightward else (i + k, i) for i in range(n - k)]


def line_gather(x, axis):
    n = lax.axis_size(axis)
    if n > LINE_MAX:
        return lax.all_gather(x, axis, axis=0, tiled=True)
    me = lax.axis_index(axis)
    parts = [x]
    sources = [me]
    for k in range(1, n):
        parts.append(lax.ppermute(x, axis, line_pairs(n, k, True)))
        sources.append(me - k)
        parts.append(lax.ppermute(x, axis, line_pairs(n, k, False)))
        sources.append(me + k)
    out = jnp.zeros((n,) + x.shape, x.dtype)
    for part, src in zip(parts, sources):
        ok = (src >= 0) & (src < n)
        out = lax.dynamic_update_index_in_dim(
            out, jnp.where(ok, part, out[jnp.clip(src, 0, n - 1)]), jnp.clip(src, 0, n - 1), 0
        )
    return out.reshape((n * x.shape[0],) + x.shape[1:])


def line_reduce_scatter(x, axis, wire):
    n = lax.axis_size(axis)
    if n > LINE_MAX or n & (n - 1):
        return lax.psum_scatter(x, axis, scatter_dimension=0, tiled=True)
    me = lax.axis_index(axis)
    rows = x.shape[0] // n
    bits = n.bit_length() - 1
    x = x.reshape((2,) * bits + (rows,) + x.shape[1:])
    for j in range(bits):
        level = 1 << j
        bit = (me // level) % 2
        keep = lax.dynamic_index_in_dim(x, bit, axis=bits - 1 - j, keepdims=False)
        send = lax.dynamic_index_in_dim(x, 1 - bit, axis=bits - 1 - j, keepdims=False).astype(wire)
        x = keep + lax.ppermute(send, axis, [(i, i ^ level) for i in range(n)]).astype(keep.dtype)
    return x


def halving_steps():
    steps = []
    for axis in ("section", "tok"):
        n = lax.axis_size(axis)
        if n & (n - 1):
            return None
        me = lax.axis_index(axis)
        level = n // 2
        while level:
            steps.append((axis, (me // level) % 2, [(i, i ^ level) for i in range(n)]))
            level //= 2
    return steps


def halving_sum(x, steps):
    for axis, bit, perm in steps:
        half = x.shape[0] // 2
        keep = lax.dynamic_slice_in_dim(x, bit * half, half, axis=0)
        send = lax.dynamic_slice_in_dim(x, (1 - bit) * half, half, axis=0)
        x = keep + lax.ppermute(send, axis, perm)
    return x


def doubling_gather(x, steps):
    for axis, bit, perm in reversed(steps):
        got = lax.ppermute(x, axis, perm)
        x = jnp.where(bit == 0, jnp.concatenate([x, got], axis=0), jnp.concatenate([got, x], axis=0))
    return x


def shards(acts, enc_weight, enc_bias, dec_weight, dec_bias, active_blocks, block_counts):
    local_enc = enc_weight[0]
    local_dec = dec_weight[:, 0, :]
    width, n_lat = local_enc.shape
    n_tok = acts.shape[1] * lax.axis_size("latent")
    width_out = local_dec.shape[1]
    tiles = n_tok // TILE
    blocks_local = n_lat // BLOCK
    most = tiles * min(active_blocks.shape[1], blocks_local)
    first_block = lax.axis_index("latent") * blocks_local

    def table(capacity):
        return pair_table(active_blocks, block_counts, first_block, blocks_local, capacity)

    def middle(capacity, pairs):
        pair_valid, count, pair_tile, pair_block = pairs
        enc_pairs = jnp.concatenate(
            [lax.dynamic_slice_in_dim(local_enc, pair_block[p] * BLOCK, BLOCK, axis=1) for p in range(capacity)], axis=1
        )
        tokens_all = lax.all_gather(acts, "latent", axis=1, tiled=True)[0]
        full = jnp.dot(tokens_all, enc_pairs.reshape(width, capacity * BLOCK), preferred_element_type=jnp.float32)
        full = full.reshape(tiles, TILE, capacity, BLOCK)
        compact = full[0]
        for t in range(1, tiles):
            compact = jnp.where((pair_tile == t)[None, :, None], full[t], compact)
        steps = halving_steps()
        if steps is None:
            shared = lax.psum_scatter(compact, ("section", "tok"), scatter_dimension=0, tiled=True)
        else:
            shared = halving_sum(compact, steps)
        bias_pairs = enc_bias.reshape(blocks_local, BLOCK)[pair_block]
        codes_part = jnp.where(
            pair_valid[None, :, None], jax.nn.relu(shared + bias_pairs[None, :, :]), 0.0
        ).astype(jnp.bfloat16)
        dec_pairs = jnp.take(local_dec.reshape(blocks_local, BLOCK, width_out), pair_block, axis=0)
        if steps is None:
            codes = lax.all_gather(codes_part, ("section", "tok"), axis=0, tiled=True)
        else:
            codes = doubling_gather(codes_part, steps)
        zero = jnp.zeros_like(codes)
        codes_full = jnp.stack([jnp.where((pair_tile == t)[None, :, None], codes, zero) for t in range(tiles)])
        return jnp.dot(
            codes_full.reshape(n_tok, capacity * BLOCK),
            dec_pairs.reshape(capacity * BLOCK, width_out),
            preferred_element_type=jnp.float32,
        )

    def middle_kernels(capacity, pairs):
        pair_valid, count, pair_tile, pair_block = pairs
        compact = sparse_call(
            encode_kernel,
            jax.ShapeDtypeStruct((capacity, TILE, BLOCK), jnp.float32),
            (width, BLOCK),
            count, pair_tile, pair_block, lax.all_gather(acts, "latent", axis=1, tiled=True)[0], local_enc,
            2 * capacity * TILE * width * BLOCK, capacity * (width * BLOCK * 2 + TILE * BLOCK * 4),
        )
        steps = halving_steps()
        if steps is None:
            shared = lax.psum_scatter(compact, ("section", "tok"), scatter_dimension=1, tiled=True)
        else:
            shared = jnp.swapaxes(halving_sum(jnp.swapaxes(compact, 0, 1), steps), 0, 1)
        bias_pairs = enc_bias.reshape(blocks_local, BLOCK)[pair_block]
        codes_part = jnp.where(
            pair_valid[:, None, None], jax.nn.relu(shared + bias_pairs[:, None, :]), 0.0
        ).astype(jnp.bfloat16)
        if steps is None:
            codes = lax.all_gather(codes_part, ("section", "tok"), axis=1, tiled=True)
        else:
            codes = jnp.swapaxes(doubling_gather(jnp.swapaxes(codes_part, 0, 1), steps), 0, 1)
        return sparse_call(
            decode_kernel,
            jax.ShapeDtypeStruct((n_tok, local_dec.shape[1]), jnp.float32),
            (BLOCK, local_dec.shape[1]),
            count, pair_tile, pair_block, codes, local_dec,
            2 * capacity * TILE * BLOCK * local_dec.shape[1], capacity * BLOCK * local_dec.shape[1] * 2,
        )

    levels = [c for c in CAPACITIES if c < most]
    if levels:
        listed = jnp.arange(active_blocks.shape[1], dtype=jnp.int32)[None, :] < block_counts[:, None]
        shard_of = active_blocks // blocks_local
        fullest = jnp.max(
            jnp.stack([jnp.sum((listed & (shard_of == s)).astype(jnp.int32)) for s in range(lax.axis_size("latent"))])
        )
        branch = sum((fullest > c).astype(jnp.int32) for c in levels)
        tables = [table(c) for c in levels + [most]]
        partial = lax.switch(
            branch,
            [functools.partial(middle if c <= GATHERED else middle_kernels, c, t) for c, t in zip(levels + [most], tables)],
        )
    else:
        partial = middle_kernels(most, table(most))
    rebuilt = line_reduce_scatter(partial, "latent", jnp.bfloat16)
    return (rebuilt + dec_bias).astype(jnp.bfloat16)[None]


def solution(mesh):
    placed = (
        P("section", "latent", "tok"),
        P("section", "tok", "latent"),
        P("latent"),
        P("latent", "section", "tok"),
        P("section", "tok"),
        P(),
        P(),
    )
    return jax.shard_map(
        shards, mesh=mesh, in_specs=placed, out_specs=P("section", "latent", "tok"), check_vma=False
    )
```

```python
import functools

import jax
import jax.numpy as jnp
from jax import lax
from jax.experimental import pallas as pl
from jax.experimental.pallas import tpu as pltpu
from jax.sharding import PartitionSpec as P

BLOCK = 128
TILE = 128


def pair_table(active_blocks, block_counts, first_block, blocks_local, capacity):
    tiles, listed = active_blocks.shape
    slot_ids = jnp.arange(listed, dtype=jnp.int32)
    local = active_blocks - first_block
    valid = ((slot_ids[None, :] < block_counts[:, None]) & (local >= 0) & (local < blocks_local)).reshape(-1)
    order = jnp.argsort(jnp.logical_not(valid).astype(jnp.int32), stable=True)[:capacity].astype(jnp.int32)
    pair_valid = valid[order]
    pair_tile = order // listed
    pair_block = jnp.where(pair_valid, local.reshape(-1)[order], 0)
    count = jnp.minimum(jnp.sum(valid.astype(jnp.int32)), capacity).reshape(1)
    return pair_valid, count, pair_tile, pair_block


DEPTH = 10


def weight_stream(n, blk_ref, source, buf, sem, compute):
    def copy(i, slot):
        return pltpu.make_async_copy(source(blk_ref[i]), buf.at[slot], sem.at[slot])

    for j in range(DEPTH):
        @pl.when(j < n)
        def _():
            copy(j, j).start()

    def body(i, carry):
        slot = i % DEPTH
        copy(i, slot).wait()
        compute(i, buf.at[slot])

        @pl.when(i + DEPTH < n)
        def _():
            copy(i + DEPTH, slot).start()

        return carry

    lax.fori_loop(0, n, body, 0)


def encode_kernel(n_ref, tile_ref, blk_ref, acts_ref, enc_hbm, out_ref, buf, sem):
    out_ref[...] = jnp.zeros(out_ref.shape, out_ref.dtype)

    def source(b):
        return enc_hbm.at[:, pl.ds(pl.multiple_of(b * BLOCK, BLOCK), BLOCK)]

    def compute(i, block):
        rows = acts_ref[pl.ds(pl.multiple_of(tile_ref[i] * TILE, TILE), TILE), :]
        out_ref[i] = jnp.dot(rows, block[...], preferred_element_type=jnp.float32)

    weight_stream(n_ref[0], blk_ref, source, buf, sem, compute)


def decode_kernel(n_ref, tile_ref, blk_ref, codes_ref, dec_hbm, out_ref, buf, sem):
    out_ref[...] = jnp.zeros(out_ref.shape, out_ref.dtype)

    def source(b):
        return dec_hbm.at[pl.ds(pl.multiple_of(b * BLOCK, BLOCK), BLOCK), :]

    def compute(i, block):
        rows = pl.ds(pl.multiple_of(tile_ref[i] * TILE, TILE), TILE)
        out_ref[rows, :] += jnp.dot(codes_ref[i], block[...], preferred_element_type=jnp.float32)

    weight_stream(n_ref[0], blk_ref, source, buf, sem, compute)


def sparse_call(kernel, out_shape, buf_shape, count, pair_tile, pair_block, dense, weight, flops, nbytes):
    smem = pl.BlockSpec(memory_space=pltpu.SMEM)
    return pl.pallas_call(
        kernel,
        out_shape=out_shape,
        in_specs=[smem, smem, smem, pl.BlockSpec(memory_space=pltpu.VMEM), pl.BlockSpec(memory_space=pl.ANY)],
        out_specs=pl.BlockSpec(memory_space=pltpu.VMEM),
        scratch_shapes=[pltpu.VMEM((DEPTH,) + buf_shape, weight.dtype), pltpu.SemaphoreType.DMA((DEPTH,))],
        cost_estimate=pl.CostEstimate(flops=flops, bytes_accessed=nbytes, transcendentals=0),
    )(count, pair_tile, pair_block, dense, weight)


LINE_MAX = 4
CAPACITIES = (12, 16, 20, 24)


def line_pairs(n, k, rightward):
    return [(i, i + k) if rightward else (i + k, i) for i in range(n - k)]


def line_gather(x, axis):
    n = lax.axis_size(axis)
    if n > LINE_MAX:
        return lax.all_gather(x, axis, axis=0, tiled=True)
    me = lax.axis_index(axis)
    parts = [x]
    sources = [me]
    for k in range(1, n):
        parts.append(lax.ppermute(x, axis, line_pairs(n, k, True)))
        sources.append(me - k)
        parts.append(lax.ppermute(x, axis, line_pairs(n, k, False)))
        sources.append(me + k)
    out = jnp.zeros((n,) + x.shape, x.dtype)
    for part, src in zip(parts, sources):
        ok = (src >= 0) & (src < n)
        out = lax.dynamic_update_index_in_dim(
            out, jnp.where(ok, part, out[jnp.clip(src, 0, n - 1)]), jnp.clip(src, 0, n - 1), 0
        )
    return out.reshape((n * x.shape[0],) + x.shape[1:])


def line_reduce_scatter(x, axis, wire):
    n = lax.axis_size(axis)
    if n > LINE_MAX or n & (n - 1):
        return lax.psum_scatter(x, axis, scatter_dimension=0, tiled=True)
    me = lax.axis_index(axis)
    rows = x.shape[0] // n
    bits = n.bit_length() - 1
    x = x.reshape((2,) * bits + (rows,) + x.shape[1:])
    for j in range(bits):
        level = 1 << j
        bit = (me // level) % 2
        keep = lax.dynamic_index_in_dim(x, bit, axis=bits - 1 - j, keepdims=False)
        send = lax.dynamic_index_in_dim(x, 1 - bit, axis=bits - 1 - j, keepdims=False).astype(wire)
        x = keep + lax.ppermute(send, axis, [(i, i ^ level) for i in range(n)]).astype(keep.dtype)
    return x


def halving_steps():
    steps = []
    for axis in ("section", "tok"):
        n = lax.axis_size(axis)
        if n & (n - 1):
            return None
        me = lax.axis_index(axis)
        level = n // 2
        while level:
            steps.append((axis, (me // level) % 2, [(i, i ^ level) for i in range(n)]))
            level //= 2
    return steps


def halving_sum(x, steps):
    for axis, bit, perm in steps:
        half = x.shape[1] // 2
        keep = lax.dynamic_slice_in_dim(x, bit * half, half, axis=1)
        send = lax.dynamic_slice_in_dim(x, (1 - bit) * half, half, axis=1)
        x = keep + lax.ppermute(send, axis, perm)
    return x


def doubling_gather(x, steps):
    for axis, bit, perm in reversed(steps):
        got = lax.ppermute(x, axis, perm)
        x = jnp.where(bit == 0, jnp.concatenate([x, got], axis=1), jnp.concatenate([got, x], axis=1))
    return x


def shards(acts, enc_weight, enc_bias, dec_weight, dec_bias, active_blocks, block_counts):
    local_enc = enc_weight[0]
    local_dec = dec_weight[:, 0, :]
    width, n_lat = local_enc.shape
    tokens_all = lax.all_gather(acts, "latent", axis=1, tiled=True)[0]
    n_tok = tokens_all.shape[0]
    tiles = n_tok // TILE
    blocks_local = n_lat // BLOCK
    most = tiles * min(active_blocks.shape[1], blocks_local)
    first_block = lax.axis_index("latent") * blocks_local

    def table(capacity):
        return pair_table(active_blocks, block_counts, first_block, blocks_local, capacity)

    def middle(capacity, pairs):
        pair_valid, count, pair_tile, pair_block = pairs
        compact = sparse_call(
            encode_kernel,
            jax.ShapeDtypeStruct((capacity, TILE, BLOCK), jnp.float32),
            (width, BLOCK),
            count, pair_tile, pair_block, tokens_all, local_enc,
            2 * capacity * TILE * width * BLOCK, capacity * (width * BLOCK * 2 + TILE * BLOCK * 4),
        )
        steps = halving_steps()
        if steps is None:
            shared = lax.psum_scatter(compact, ("section", "tok"), scatter_dimension=1, tiled=True)
        else:
            shared = halving_sum(compact, steps)
        bias_pairs = enc_bias.reshape(blocks_local, BLOCK)[pair_block]
        codes_part = jnp.where(
            pair_valid[:, None, None], jax.nn.relu(shared + bias_pairs[:, None, :]), 0.0
        ).astype(jnp.bfloat16)
        if steps is None:
            codes = lax.all_gather(codes_part, ("section", "tok"), axis=1, tiled=True)
        else:
            codes = doubling_gather(codes_part, steps)
        return sparse_call(
            decode_kernel,
            jax.ShapeDtypeStruct((n_tok, local_dec.shape[1]), jnp.float32),
            (BLOCK, local_dec.shape[1]),
            count, pair_tile, pair_block, codes, local_dec,
            2 * capacity * TILE * BLOCK * local_dec.shape[1], capacity * BLOCK * local_dec.shape[1] * 2,
        )

    levels = [c for c in CAPACITIES if c < most]
    if levels:
        listed = jnp.arange(active_blocks.shape[1], dtype=jnp.int32)[None, :] < block_counts[:, None]
        shard_of = active_blocks // blocks_local
        fullest = jnp.max(
            jnp.stack([jnp.sum((listed & (shard_of == s)).astype(jnp.int32)) for s in range(lax.axis_size("latent"))])
        )
        branch = sum((fullest > c).astype(jnp.int32) for c in levels)
        tables = [table(c) for c in levels + [most]]
        partial = lax.switch(branch, [functools.partial(middle, c, t) for c, t in zip(levels + [most], tables)])
    else:
        partial = middle(most, table(most))
    rebuilt = line_reduce_scatter(partial, "latent", jnp.bfloat16)
    return (rebuilt + dec_bias).astype(jnp.bfloat16)[None]


def solution(mesh):
    placed = (
        P("section", "latent", "tok"),
        P("section", "tok", "latent"),
        P("latent"),
        P("latent", "section", "tok"),
        P("section", "tok"),
        P(),
        P(),
    )
    return jax.shard_map(
        shards, mesh=mesh, in_specs=placed, out_specs=P("section", "latent", "tok"), check_vma=False
    )
```

```python
import functools

import jax
import jax.numpy as jnp
from jax import lax
from jax.experimental import pallas as pl
from jax.experimental.pallas import tpu as pltpu
from jax.sharding import PartitionSpec as P

BLOCK = 128
TILE = 128


def pair_table(active_blocks, block_counts, first_block, blocks_local, capacity):
    tiles, listed = active_blocks.shape
    slot_ids = jnp.arange(listed, dtype=jnp.int32)
    local = active_blocks - first_block
    valid = ((slot_ids[None, :] < block_counts[:, None]) & (local >= 0) & (local < blocks_local)).reshape(-1)
    order = jnp.argsort(jnp.logical_not(valid).astype(jnp.int32), stable=True)[:capacity].astype(jnp.int32)
    pair_valid = valid[order]
    pair_tile = order // listed
    pair_block = jnp.where(pair_valid, local.reshape(-1)[order], 0)
    count = jnp.minimum(jnp.sum(valid.astype(jnp.int32)), capacity).reshape(1)
    return pair_valid, count, pair_tile, pair_block


DEPTH = 10


def weight_stream(n, blk_ref, source, buf, sem, compute):
    def copy(i, slot):
        return pltpu.make_async_copy(source(blk_ref[i]), buf.at[slot], sem.at[slot])

    for j in range(DEPTH):
        @pl.when(j < n)
        def _():
            copy(j, j).start()

    def body(i, carry):
        slot = i % DEPTH
        copy(i, slot).wait()
        compute(i, buf.at[slot])

        @pl.when(i + DEPTH < n)
        def _():
            copy(i + DEPTH, slot).start()

        return carry

    lax.fori_loop(0, n, body, 0)


def encode_kernel(n_ref, tile_ref, blk_ref, acts_ref, enc_hbm, out_ref, buf, sem):
    out_ref[...] = jnp.zeros(out_ref.shape, out_ref.dtype)

    def source(b):
        return enc_hbm.at[:, pl.ds(pl.multiple_of(b * BLOCK, BLOCK), BLOCK)]

    def compute(i, block):
        rows = acts_ref[pl.ds(pl.multiple_of(tile_ref[i] * TILE, TILE), TILE), :]
        out_ref[i] = jnp.dot(rows, block[...], preferred_element_type=jnp.float32)

    weight_stream(n_ref[0], blk_ref, source, buf, sem, compute)


def decode_kernel(n_ref, tile_ref, blk_ref, codes_ref, dec_hbm, out_ref, buf, sem):
    out_ref[...] = jnp.zeros(out_ref.shape, out_ref.dtype)

    def source(b):
        return dec_hbm.at[pl.ds(pl.multiple_of(b * BLOCK, BLOCK), BLOCK), :]

    def compute(i, block):
        rows = pl.ds(pl.multiple_of(tile_ref[i] * TILE, TILE), TILE)
        out_ref[rows, :] += jnp.dot(codes_ref[i], block[...], preferred_element_type=jnp.float32)

    weight_stream(n_ref[0], blk_ref, source, buf, sem, compute)


def sparse_call(kernel, out_shape, buf_shape, count, pair_tile, pair_block, dense, weight, flops, nbytes):
    smem = pl.BlockSpec(memory_space=pltpu.SMEM)
    return pl.pallas_call(
        kernel,
        out_shape=out_shape,
        in_specs=[smem, smem, smem, pl.BlockSpec(memory_space=pltpu.VMEM), pl.BlockSpec(memory_space=pl.ANY)],
        out_specs=pl.BlockSpec(memory_space=pltpu.VMEM),
        scratch_shapes=[pltpu.VMEM((DEPTH,) + buf_shape, weight.dtype), pltpu.SemaphoreType.DMA((DEPTH,))],
        cost_estimate=pl.CostEstimate(flops=flops, bytes_accessed=nbytes, transcendentals=0),
    )(count, pair_tile, pair_block, dense, weight)


LINE_MAX = 4
CAPACITIES = (12, 16, 20, 24)


def line_pairs(n, k, rightward):
    return [(i, i + k) if rightward else (i + k, i) for i in range(n - k)]


def line_gather(x, axis):
    n = lax.axis_size(axis)
    if n > LINE_MAX:
        return lax.all_gather(x, axis, axis=0, tiled=True)
    me = lax.axis_index(axis)
    parts = [x]
    sources = [me]
    for k in range(1, n):
        parts.append(lax.ppermute(x, axis, line_pairs(n, k, True)))
        sources.append(me - k)
        parts.append(lax.ppermute(x, axis, line_pairs(n, k, False)))
        sources.append(me + k)
    out = jnp.zeros((n,) + x.shape, x.dtype)
    for part, src in zip(parts, sources):
        ok = (src >= 0) & (src < n)
        out = lax.dynamic_update_index_in_dim(
            out, jnp.where(ok, part, out[jnp.clip(src, 0, n - 1)]), jnp.clip(src, 0, n - 1), 0
        )
    return out.reshape((n * x.shape[0],) + x.shape[1:])


def shift_gather(x, axis):
    n = lax.axis_size(axis)
    if n > LINE_MAX:
        return lax.all_gather(x, axis, axis=0, tiled=True)
    me = lax.axis_index(axis)
    out = jnp.zeros((n,) + x.shape, x.dtype)
    out = lax.dynamic_update_index_in_dim(out, x, me, 0)
    for k in range(1, n):
        got = lax.ppermute(x, axis, [(i, (i + k) % n) for i in range(n)])
        out = lax.dynamic_update_index_in_dim(out, got, (me - k) % n, 0)
    return out.reshape((n * x.shape[0],) + x.shape[1:])


def line_reduce_scatter(x, axis, wire):
    n = lax.axis_size(axis)
    if n > LINE_MAX or n & (n - 1):
        return lax.psum_scatter(x, axis, scatter_dimension=0, tiled=True)
    me = lax.axis_index(axis)
    rows = x.shape[0] // n
    bits = n.bit_length() - 1
    x = x.reshape((2,) * bits + (rows,) + x.shape[1:])
    for j in range(bits):
        level = 1 << j
        bit = (me // level) % 2
        keep = lax.dynamic_index_in_dim(x, bit, axis=bits - 1 - j, keepdims=False)
        send = lax.dynamic_index_in_dim(x, 1 - bit, axis=bits - 1 - j, keepdims=False).astype(wire)
        x = keep + lax.ppermute(send, axis, [(i, i ^ level) for i in range(n)]).astype(keep.dtype)
    return x


def halving_steps():
    steps = []
    for axis in ("section", "tok"):
        n = lax.axis_size(axis)
        if n & (n - 1):
            return None
        me = lax.axis_index(axis)
        level = n // 2
        while level:
            steps.append((axis, (me // level) % 2, [(i, i ^ level) for i in range(n)]))
            level //= 2
    return steps


def halving_sum(x, steps):
    for axis, bit, perm in steps:
        half = x.shape[1] // 2
        keep = lax.dynamic_slice_in_dim(x, bit * half, half, axis=1)
        send = lax.dynamic_slice_in_dim(x, (1 - bit) * half, half, axis=1)
        x = keep + lax.ppermute(send, axis, perm)
    return x


def doubling_gather(x, steps):
    for axis, bit, perm in reversed(steps):
        got = lax.ppermute(x, axis, perm)
        x = jnp.where(bit == 0, jnp.concatenate([x, got], axis=1), jnp.concatenate([got, x], axis=1))
    return x


def shards(acts, enc_weight, enc_bias, dec_weight, dec_bias, active_blocks, block_counts):
    local_enc = enc_weight[0]
    local_dec = dec_weight[:, 0, :]
    width, n_lat = local_enc.shape
    tokens_all = shift_gather(acts[0], "latent")
    n_tok = tokens_all.shape[0]
    tiles = n_tok // TILE
    blocks_local = n_lat // BLOCK
    most = tiles * min(active_blocks.shape[1], blocks_local)
    first_block = lax.axis_index("latent") * blocks_local

    def table(capacity):
        return pair_table(active_blocks, block_counts, first_block, blocks_local, capacity)

    def middle(capacity, pairs):
        pair_valid, count, pair_tile, pair_block = pairs
        compact = sparse_call(
            encode_kernel,
            jax.ShapeDtypeStruct((capacity, TILE, BLOCK), jnp.float32),
            (width, BLOCK),
            count, pair_tile, pair_block, tokens_all, local_enc,
            2 * capacity * TILE * width * BLOCK, capacity * (width * BLOCK * 2 + TILE * BLOCK * 4),
        )
        steps = halving_steps()
        if steps is None:
            shared = lax.psum_scatter(compact, ("section", "tok"), scatter_dimension=1, tiled=True)
        else:
            shared = halving_sum(compact, steps)
        bias_pairs = enc_bias.reshape(blocks_local, BLOCK)[pair_block]
        codes_part = jnp.where(
            pair_valid[:, None, None], jax.nn.relu(shared + bias_pairs[:, None, :]), 0.0
        ).astype(jnp.bfloat16)
        if steps is None:
            codes = lax.all_gather(codes_part, ("section", "tok"), axis=1, tiled=True)
        else:
            codes = doubling_gather(codes_part, steps)
        return sparse_call(
            decode_kernel,
            jax.ShapeDtypeStruct((n_tok, local_dec.shape[1]), jnp.float32),
            (BLOCK, local_dec.shape[1]),
            count, pair_tile, pair_block, codes, local_dec,
            2 * capacity * TILE * BLOCK * local_dec.shape[1], capacity * BLOCK * local_dec.shape[1] * 2,
        )

    levels = [c for c in CAPACITIES if c < most]
    if levels:
        listed = jnp.arange(active_blocks.shape[1], dtype=jnp.int32)[None, :] < block_counts[:, None]
        shard_of = active_blocks // blocks_local
        fullest = jnp.max(
            jnp.stack([jnp.sum((listed & (shard_of == s)).astype(jnp.int32)) for s in range(lax.axis_size("latent"))])
        )
        branch = sum((fullest > c).astype(jnp.int32) for c in levels)
        tables = [table(c) for c in levels + [most]]
        partial = lax.switch(branch, [functools.partial(middle, c, t) for c, t in zip(levels + [most], tables)])
    else:
        partial = middle(most, table(most))
    rebuilt = line_reduce_scatter(partial, "latent", jnp.bfloat16)
    return (rebuilt + dec_bias).astype(jnp.bfloat16)[None]


def solution(mesh):
    placed = (
        P("section", "latent", "tok"),
        P("section", "tok", "latent"),
        P("latent"),
        P("latent", "section", "tok"),
        P("section", "tok"),
        P(),
        P(),
    )
    return jax.shard_map(
        shards, mesh=mesh, in_specs=placed, out_specs=P("section", "latent", "tok"), check_vma=False
    )
```

```python
import functools

import jax
import jax.numpy as jnp
from jax import lax
from jax.experimental import pallas as pl
from jax.experimental.pallas import tpu as pltpu
from jax.sharding import PartitionSpec as P

BLOCK = 128
TILE = 128


def pair_table(active_blocks, block_counts, first_block, blocks_local, capacity):
    tiles, listed = active_blocks.shape
    slot_ids = jnp.arange(listed, dtype=jnp.int32)
    local = active_blocks - first_block
    valid = ((slot_ids[None, :] < block_counts[:, None]) & (local >= 0) & (local < blocks_local)).reshape(-1)
    order = jnp.argsort(jnp.logical_not(valid).astype(jnp.int32), stable=True)[:capacity].astype(jnp.int32)
    pair_valid = valid[order]
    pair_tile = order // listed
    pair_block = jnp.where(pair_valid, local.reshape(-1)[order], 0)
    count = jnp.minimum(jnp.sum(valid.astype(jnp.int32)), capacity).reshape(1)
    return pair_valid, count, pair_tile, pair_block


DEPTH = 10


def weight_stream(n, blk_ref, source, buf, sem, compute):
    def copy(i, slot):
        return pltpu.make_async_copy(source(blk_ref[i]), buf.at[slot], sem.at[slot])

    for j in range(DEPTH):
        @pl.when(j < n)
        def _():
            copy(j, j).start()

    def body(i, carry):
        slot = i % DEPTH
        copy(i, slot).wait()
        compute(i, buf.at[slot])

        @pl.when(i + DEPTH < n)
        def _():
            copy(i + DEPTH, slot).start()

        return carry

    lax.fori_loop(0, n, body, 0)


def encode_kernel(n_ref, tile_ref, blk_ref, acts_ref, enc_hbm, out_ref, buf, sem):
    out_ref[...] = jnp.zeros(out_ref.shape, out_ref.dtype)

    def source(b):
        return enc_hbm.at[:, pl.ds(pl.multiple_of(b * BLOCK, BLOCK), BLOCK)]

    def compute(i, block):
        rows = acts_ref[pl.ds(pl.multiple_of(tile_ref[i] * TILE, TILE), TILE), :]
        out_ref[i] = jnp.dot(rows, block[...], preferred_element_type=jnp.float32)

    weight_stream(n_ref[0], blk_ref, source, buf, sem, compute)


def decode_kernel(n_ref, tile_ref, blk_ref, codes_ref, dec_hbm, out_ref, buf, sem):
    out_ref[...] = jnp.zeros(out_ref.shape, out_ref.dtype)

    def source(b):
        return dec_hbm.at[pl.ds(pl.multiple_of(b * BLOCK, BLOCK), BLOCK), :]

    def compute(i, block):
        rows = pl.ds(pl.multiple_of(tile_ref[i] * TILE, TILE), TILE)
        out_ref[rows, :] += jnp.dot(codes_ref[i], block[...], preferred_element_type=jnp.float32)

    weight_stream(n_ref[0], blk_ref, source, buf, sem, compute)


def sparse_call(kernel, out_shape, buf_shape, count, pair_tile, pair_block, dense, weight, flops, nbytes):
    smem = pl.BlockSpec(memory_space=pltpu.SMEM)
    return pl.pallas_call(
        kernel,
        out_shape=out_shape,
        in_specs=[smem, smem, smem, pl.BlockSpec(memory_space=pltpu.VMEM), pl.BlockSpec(memory_space=pl.ANY)],
        out_specs=pl.BlockSpec(memory_space=pltpu.VMEM),
        scratch_shapes=[pltpu.VMEM((DEPTH,) + buf_shape, weight.dtype), pltpu.SemaphoreType.DMA((DEPTH,))],
        cost_estimate=pl.CostEstimate(flops=flops, bytes_accessed=nbytes, transcendentals=0),
    )(count, pair_tile, pair_block, dense, weight)


LINE_MAX = 4
CAPACITIES = (12, 16, 20, 24)


def line_pairs(n, k, rightward):
    return [(i, i + k) if rightward else (i + k, i) for i in range(n - k)]


def line_gather(x, axis):
    n = lax.axis_size(axis)
    if n > LINE_MAX:
        return lax.all_gather(x, axis, axis=0, tiled=True)
    me = lax.axis_index(axis)
    parts = [x]
    sources = [me]
    for k in range(1, n):
        parts.append(lax.ppermute(x, axis, line_pairs(n, k, True)))
        sources.append(me - k)
        parts.append(lax.ppermute(x, axis, line_pairs(n, k, False)))
        sources.append(me + k)
    out = jnp.zeros((n,) + x.shape, x.dtype)
    for part, src in zip(parts, sources):
        ok = (src >= 0) & (src < n)
        out = lax.dynamic_update_index_in_dim(
            out, jnp.where(ok, part, out[jnp.clip(src, 0, n - 1)]), jnp.clip(src, 0, n - 1), 0
        )
    return out.reshape((n * x.shape[0],) + x.shape[1:])


def shift_gather(x, axis):
    n = lax.axis_size(axis)
    if n > LINE_MAX:
        return lax.all_gather(x, axis, axis=0, tiled=True)
    me = lax.axis_index(axis)
    out = jnp.zeros((n,) + x.shape, x.dtype)
    out = lax.dynamic_update_index_in_dim(out, x, me, 0)
    for k in range(1, n):
        got = lax.ppermute(x, axis, [(i, (i + k) % n) for i in range(n)])
        out = lax.dynamic_update_index_in_dim(out, got, (me - k) % n, 0)
    return out.reshape((n * x.shape[0],) + x.shape[1:])


def line_reduce_scatter(x, axis, wire):
    n = lax.axis_size(axis)
    if n > LINE_MAX or n & (n - 1):
        return lax.psum_scatter(x, axis, scatter_dimension=0, tiled=True)
    bits = n.bit_length() - 1
    cols = x.shape[1] // 2
    halves = [x[:, :cols], x[:, cols:]]
    orders = [list(range(bits)), list(reversed(range(bits)))]
    return jnp.concatenate([halving_rows(h, axis, wire, o) for h, o in zip(halves, orders)], axis=1)


def halving_rows(x, axis, wire, order):
    n = lax.axis_size(axis)
    me = lax.axis_index(axis)
    bits = len(order)
    rows = x.shape[0] // n
    x = x.reshape((2,) * bits + (rows,) + x.shape[1:])
    dims = list(reversed(range(bits)))
    for j in order:
        level = 1 << j
        bit = (me // level) % 2
        at = dims.index(j)
        dims.remove(j)
        keep = lax.dynamic_index_in_dim(x, bit, axis=at, keepdims=False)
        send = lax.dynamic_index_in_dim(x, 1 - bit, axis=at, keepdims=False).astype(wire)
        x = keep + lax.ppermute(send, axis, [(i, i ^ level) for i in range(n)]).astype(keep.dtype)
    return x


def halving_steps():
    steps = []
    for axis in ("section", "tok"):
        n = lax.axis_size(axis)
        if n & (n - 1):
            return None
        me = lax.axis_index(axis)
        level = n // 2
        while level:
            steps.append((axis, (me // level) % 2, [(i, i ^ level) for i in range(n)]))
            level //= 2
    return steps


def halving_sum(x, steps):
    for axis, bit, perm in steps:
        half = x.shape[1] // 2
        keep = lax.dynamic_slice_in_dim(x, bit * half, half, axis=1)
        send = lax.dynamic_slice_in_dim(x, (1 - bit) * half, half, axis=1)
        x = keep + lax.ppermute(send, axis, perm)
    return x


def doubling_gather(x, steps):
    for axis, bit, perm in reversed(steps):
        got = lax.ppermute(x, axis, perm)
        x = jnp.where(bit == 0, jnp.concatenate([x, got], axis=1), jnp.concatenate([got, x], axis=1))
    return x


def shards(acts, enc_weight, enc_bias, dec_weight, dec_bias, active_blocks, block_counts):
    local_enc = enc_weight[0]
    local_dec = dec_weight[:, 0, :]
    width, n_lat = local_enc.shape
    tokens_all = shift_gather(acts[0], "latent")
    n_tok = tokens_all.shape[0]
    tiles = n_tok // TILE
    blocks_local = n_lat // BLOCK
    most = tiles * min(active_blocks.shape[1], blocks_local)
    first_block = lax.axis_index("latent") * blocks_local

    def table(capacity):
        return pair_table(active_blocks, block_counts, first_block, blocks_local, capacity)

    def middle(capacity, pairs):
        pair_valid, count, pair_tile, pair_block = pairs
        compact = sparse_call(
            encode_kernel,
            jax.ShapeDtypeStruct((capacity, TILE, BLOCK), jnp.float32),
            (width, BLOCK),
            count, pair_tile, pair_block, tokens_all, local_enc,
            2 * capacity * TILE * width * BLOCK, capacity * (width * BLOCK * 2 + TILE * BLOCK * 4),
        )
        steps = halving_steps()
        if steps is None:
            shared = lax.psum_scatter(compact, ("section", "tok"), scatter_dimension=1, tiled=True)
        else:
            shared = halving_sum(compact, steps)
        bias_pairs = enc_bias.reshape(blocks_local, BLOCK)[pair_block]
        codes_part = jnp.where(
            pair_valid[:, None, None], jax.nn.relu(shared + bias_pairs[:, None, :]), 0.0
        ).astype(jnp.bfloat16)
        if steps is None:
            codes = lax.all_gather(codes_part, ("section", "tok"), axis=1, tiled=True)
        else:
            codes = doubling_gather(codes_part, steps)
        return sparse_call(
            decode_kernel,
            jax.ShapeDtypeStruct((n_tok, local_dec.shape[1]), jnp.float32),
            (BLOCK, local_dec.shape[1]),
            count, pair_tile, pair_block, codes, local_dec,
            2 * capacity * TILE * BLOCK * local_dec.shape[1], capacity * BLOCK * local_dec.shape[1] * 2,
        )

    levels = [c for c in CAPACITIES if c < most]
    if levels:
        listed = jnp.arange(active_blocks.shape[1], dtype=jnp.int32)[None, :] < block_counts[:, None]
        shard_of = active_blocks // blocks_local
        fullest = jnp.max(
            jnp.stack([jnp.sum((listed & (shard_of == s)).astype(jnp.int32)) for s in range(lax.axis_size("latent"))])
        )
        branch = sum((fullest > c).astype(jnp.int32) for c in levels)
        tables = [table(c) for c in levels + [most]]
        partial = lax.switch(branch, [functools.partial(middle, c, t) for c, t in zip(levels + [most], tables)])
    else:
        partial = middle(most, table(most))
    rebuilt = line_reduce_scatter(partial, "latent", jnp.bfloat16)
    return (rebuilt + dec_bias).astype(jnp.bfloat16)[None]


def solution(mesh):
    placed = (
        P("section", "latent", "tok"),
        P("section", "tok", "latent"),
        P("latent"),
        P("latent", "section", "tok"),
        P("section", "tok"),
        P(),
        P(),
    )
    return jax.shard_map(
        shards, mesh=mesh, in_specs=placed, out_specs=P("section", "latent", "tok"), check_vma=False
    )
```

```python
import functools

import jax
import jax.numpy as jnp
from jax import lax
from jax.experimental import pallas as pl
from jax.experimental.pallas import tpu as pltpu
from jax.sharding import PartitionSpec as P

BLOCK = 128
TILE = 128


def pair_table(active_blocks, block_counts, first_block, blocks_local, capacity):
    tiles, listed = active_blocks.shape
    slot_ids = jnp.arange(listed, dtype=jnp.int32)
    local = active_blocks - first_block
    valid = ((slot_ids[None, :] < block_counts[:, None]) & (local >= 0) & (local < blocks_local)).reshape(-1)
    order = jnp.argsort(jnp.logical_not(valid).astype(jnp.int32), stable=True)[:capacity].astype(jnp.int32)
    pair_valid = valid[order]
    pair_tile = order // listed
    pair_block = jnp.where(pair_valid, local.reshape(-1)[order], 0)
    count = jnp.minimum(jnp.sum(valid.astype(jnp.int32)), capacity).reshape(1)
    return pair_valid, count, pair_tile, pair_block


DEPTH = 16


def weight_stream(n, blk_ref, source, buf, sem, compute):
    def copy(i, slot):
        return pltpu.make_async_copy(source(blk_ref[i]), buf.at[slot], sem.at[slot])

    for j in range(DEPTH):
        @pl.when(j < n)
        def _():
            copy(j, j).start()

    def body(i, carry):
        slot = i % DEPTH
        copy(i, slot).wait()
        compute(i, buf.at[slot])

        @pl.when(i + DEPTH < n)
        def _():
            copy(i + DEPTH, slot).start()

        return carry

    lax.fori_loop(0, n, body, 0)


def encode_kernel(n_ref, tile_ref, blk_ref, acts_ref, enc_hbm, out_ref, buf, sem):
    out_ref[...] = jnp.zeros(out_ref.shape, out_ref.dtype)

    def source(b):
        return enc_hbm.at[:, pl.ds(pl.multiple_of(b * BLOCK, BLOCK), BLOCK)]

    def compute(i, block):
        rows = acts_ref[pl.ds(pl.multiple_of(tile_ref[i] * TILE, TILE), TILE), :]
        out_ref[i] = jnp.dot(rows, block[...], preferred_element_type=jnp.float32)

    weight_stream(n_ref[0], blk_ref, source, buf, sem, compute)


def decode_kernel(n_ref, tile_ref, blk_ref, codes_ref, dec_hbm, out_ref, buf, sem):
    out_ref[...] = jnp.zeros(out_ref.shape, out_ref.dtype)

    def source(b):
        return dec_hbm.at[pl.ds(pl.multiple_of(b * BLOCK, BLOCK), BLOCK), :]

    def compute(i, block):
        rows = pl.ds(pl.multiple_of(tile_ref[i] * TILE, TILE), TILE)
        out_ref[rows, :] += jnp.dot(codes_ref[i], block[...], preferred_element_type=jnp.float32)

    weight_stream(n_ref[0], blk_ref, source, buf, sem, compute)


def sparse_call(kernel, out_shape, buf_shape, count, pair_tile, pair_block, dense, weight, flops, nbytes):
    smem = pl.BlockSpec(memory_space=pltpu.SMEM)
    return pl.pallas_call(
        kernel,
        out_shape=out_shape,
        in_specs=[smem, smem, smem, pl.BlockSpec(memory_space=pltpu.VMEM), pl.BlockSpec(memory_space=pl.ANY)],
        out_specs=pl.BlockSpec(memory_space=pltpu.VMEM),
        scratch_shapes=[pltpu.VMEM((DEPTH,) + buf_shape, weight.dtype), pltpu.SemaphoreType.DMA((DEPTH,))],
        cost_estimate=pl.CostEstimate(flops=flops, bytes_accessed=nbytes, transcendentals=0),
    )(count, pair_tile, pair_block, dense, weight)


LINE_MAX = 4
CAPACITIES = (12, 16, 20, 24)


def line_pairs(n, k, rightward):
    return [(i, i + k) if rightward else (i + k, i) for i in range(n - k)]


def line_gather(x, axis):
    n = lax.axis_size(axis)
    if n > LINE_MAX:
        return lax.all_gather(x, axis, axis=0, tiled=True)
    me = lax.axis_index(axis)
    parts = [x]
    sources = [me]
    for k in range(1, n):
        parts.append(lax.ppermute(x, axis, line_pairs(n, k, True)))
        sources.append(me - k)
        parts.append(lax.ppermute(x, axis, line_pairs(n, k, False)))
        sources.append(me + k)
    out = jnp.zeros((n,) + x.shape, x.dtype)
    for part, src in zip(parts, sources):
        ok = (src >= 0) & (src < n)
        out = lax.dynamic_update_index_in_dim(
            out, jnp.where(ok, part, out[jnp.clip(src, 0, n - 1)]), jnp.clip(src, 0, n - 1), 0
        )
    return out.reshape((n * x.shape[0],) + x.shape[1:])


def shift_gather(x, axis):
    n = lax.axis_size(axis)
    if n > LINE_MAX:
        return lax.all_gather(x, axis, axis=0, tiled=True)
    me = lax.axis_index(axis)
    out = jnp.zeros((n,) + x.shape, x.dtype)
    out = lax.dynamic_update_index_in_dim(out, x, me, 0)
    for k in range(1, n):
        got = lax.ppermute(x, axis, [(i, (i + k) % n) for i in range(n)])
        out = lax.dynamic_update_index_in_dim(out, got, (me - k) % n, 0)
    return out.reshape((n * x.shape[0],) + x.shape[1:])


def line_reduce_scatter(x, axis, wire):
    n = lax.axis_size(axis)
    if n > LINE_MAX or n & (n - 1):
        return lax.psum_scatter(x, axis, scatter_dimension=0, tiled=True)
    me = lax.axis_index(axis)
    rows = x.shape[0] // n
    bits = n.bit_length() - 1
    x = x.reshape((2,) * bits + (rows,) + x.shape[1:])
    for j in range(bits):
        level = 1 << j
        bit = (me // level) % 2
        keep = lax.dynamic_index_in_dim(x, bit, axis=bits - 1 - j, keepdims=False)
        send = lax.dynamic_index_in_dim(x, 1 - bit, axis=bits - 1 - j, keepdims=False).astype(wire)
        x = keep + lax.ppermute(send, axis, [(i, i ^ level) for i in range(n)]).astype(keep.dtype)
    return x


def halving_steps():
    steps = []
    for axis in ("section", "tok"):
        n = lax.axis_size(axis)
        if n & (n - 1):
            return None
        me = lax.axis_index(axis)
        level = n // 2
        while level:
            steps.append((axis, (me // level) % 2, [(i, i ^ level) for i in range(n)]))
            level //= 2
    return steps


def halving_sum(x, steps):
    for axis, bit, perm in steps:
        half = x.shape[1] // 2
        keep = lax.dynamic_slice_in_dim(x, bit * half, half, axis=1)
        send = lax.dynamic_slice_in_dim(x, (1 - bit) * half, half, axis=1)
        x = keep + lax.ppermute(send, axis, perm)
    return x


def doubling_gather(x, steps):
    for axis, bit, perm in reversed(steps):
        got = lax.ppermute(x, axis, perm)
        x = jnp.where(bit == 0, jnp.concatenate([x, got], axis=1), jnp.concatenate([got, x], axis=1))
    return x


def shards(acts, enc_weight, enc_bias, dec_weight, dec_bias, active_blocks, block_counts):
    local_enc = enc_weight[0]
    local_dec = dec_weight[:, 0, :]
    width, n_lat = local_enc.shape
    tokens_all = shift_gather(acts[0], "latent")
    n_tok = tokens_all.shape[0]
    tiles = n_tok // TILE
    blocks_local = n_lat // BLOCK
    most = tiles * min(active_blocks.shape[1], blocks_local)
    first_block = lax.axis_index("latent") * blocks_local

    def table(capacity):
        return pair_table(active_blocks, block_counts, first_block, blocks_local, capacity)

    def middle(capacity, pairs):
        pair_valid, count, pair_tile, pair_block = pairs
        compact = sparse_call(
            encode_kernel,
            jax.ShapeDtypeStruct((capacity, TILE, BLOCK), jnp.float32),
            (width, BLOCK),
            count, pair_tile, pair_block, tokens_all, local_enc,
            2 * capacity * TILE * width * BLOCK, capacity * (width * BLOCK * 2 + TILE * BLOCK * 4),
        )
        steps = halving_steps()
        if steps is None:
            shared = lax.psum_scatter(compact, ("section", "tok"), scatter_dimension=1, tiled=True)
        else:
            shared = halving_sum(compact, steps)
        bias_pairs = enc_bias.reshape(blocks_local, BLOCK)[pair_block]
        codes_part = jnp.where(
            pair_valid[:, None, None], jax.nn.relu(shared + bias_pairs[:, None, :]), 0.0
        ).astype(jnp.bfloat16)
        if steps is None:
            codes = lax.all_gather(codes_part, ("section", "tok"), axis=1, tiled=True)
        else:
            codes = doubling_gather(codes_part, steps)
        return sparse_call(
            decode_kernel,
            jax.ShapeDtypeStruct((n_tok, local_dec.shape[1]), jnp.float32),
            (BLOCK, local_dec.shape[1]),
            count, pair_tile, pair_block, codes, local_dec,
            2 * capacity * TILE * BLOCK * local_dec.shape[1], capacity * BLOCK * local_dec.shape[1] * 2,
        )

    levels = [c for c in CAPACITIES if c < most]
    if levels:
        listed = jnp.arange(active_blocks.shape[1], dtype=jnp.int32)[None, :] < block_counts[:, None]
        shard_of = active_blocks // blocks_local
        fullest = jnp.max(
            jnp.stack([jnp.sum((listed & (shard_of == s)).astype(jnp.int32)) for s in range(lax.axis_size("latent"))])
        )
        branch = sum((fullest > c).astype(jnp.int32) for c in levels)
        tables = [table(c) for c in levels + [most]]
        partial = lax.switch(branch, [functools.partial(middle, c, t) for c, t in zip(levels + [most], tables)])
    else:
        partial = middle(most, table(most))
    rebuilt = line_reduce_scatter(partial, "latent", jnp.bfloat16)
    return (rebuilt + dec_bias).astype(jnp.bfloat16)[None]


def solution(mesh):
    placed = (
        P("section", "latent", "tok"),
        P("section", "tok", "latent"),
        P("latent"),
        P("latent", "section", "tok"),
        P("section", "tok"),
        P(),
        P(),
    )
    return jax.shard_map(
        shards, mesh=mesh, in_specs=placed, out_specs=P("section", "latent", "tok"), check_vma=False
    )
```

```python
import functools

import jax
import jax.numpy as jnp
from jax import lax
from jax.experimental import pallas as pl
from jax.experimental.pallas import tpu as pltpu
from jax.sharding import PartitionSpec as P

BLOCK = 128
TILE = 128


def pair_table(active_blocks, block_counts, first_block, blocks_local, capacity):
    tiles, listed = active_blocks.shape
    slot_ids = jnp.arange(listed, dtype=jnp.int32)
    local = active_blocks - first_block
    valid = ((slot_ids[None, :] < block_counts[:, None]) & (local >= 0) & (local < blocks_local)).reshape(-1)
    order = jnp.argsort(jnp.logical_not(valid).astype(jnp.int32), stable=True)[:capacity].astype(jnp.int32)
    pair_valid = valid[order]
    pair_tile = order // listed
    pair_block = jnp.where(pair_valid, local.reshape(-1)[order], 0)
    count = jnp.minimum(jnp.sum(valid.astype(jnp.int32)), capacity).reshape(1)
    return pair_valid, count, pair_tile, pair_block


DEPTH = 10


def weight_stream(n, blk_ref, source, buf, sem, compute):
    def copy(i, slot):
        return pltpu.make_async_copy(source(blk_ref[i]), buf.at[slot], sem.at[slot])

    for j in range(DEPTH):
        @pl.when(j < n)
        def _():
            copy(j, j).start()

    def body(i, carry):
        slot = i % DEPTH
        copy(i, slot).wait()
        compute(i, buf.at[slot])

        @pl.when(i + DEPTH < n)
        def _():
            copy(i + DEPTH, slot).start()

        return carry

    lax.fori_loop(0, n, body, 0)


def encode_kernel(n_ref, tile_ref, blk_ref, acts_ref, enc_hbm, out_ref, buf, sem):
    out_ref[...] = jnp.zeros(out_ref.shape, out_ref.dtype)

    def source(b):
        return enc_hbm.at[:, pl.ds(pl.multiple_of(b * BLOCK, BLOCK), BLOCK)]

    def compute(i, block):
        rows = acts_ref[pl.ds(pl.multiple_of(tile_ref[i] * TILE, TILE), TILE), :]
        out_ref[i] = jnp.dot(rows, block[...], preferred_element_type=jnp.float32)

    weight_stream(n_ref[0], blk_ref, source, buf, sem, compute)


def decode_kernel(n_ref, tile_ref, blk_ref, codes_ref, dec_hbm, out_ref, buf, sem):
    out_ref[...] = jnp.zeros(out_ref.shape, out_ref.dtype)

    def source(b):
        return dec_hbm.at[pl.ds(pl.multiple_of(b * BLOCK, BLOCK), BLOCK), :]

    def compute(i, block):
        rows = pl.ds(pl.multiple_of(tile_ref[i] * TILE, TILE), TILE)
        out_ref[rows, :] += jnp.dot(codes_ref[i], block[...], preferred_element_type=jnp.float32)

    weight_stream(n_ref[0], blk_ref, source, buf, sem, compute)


def sparse_call(kernel, out_shape, buf_shape, count, pair_tile, pair_block, dense, weight, flops, nbytes):
    smem = pl.BlockSpec(memory_space=pltpu.SMEM)
    return pl.pallas_call(
        kernel,
        out_shape=out_shape,
        in_specs=[smem, smem, smem, pl.BlockSpec(memory_space=pltpu.VMEM), pl.BlockSpec(memory_space=pl.ANY)],
        out_specs=pl.BlockSpec(memory_space=pltpu.VMEM),
        scratch_shapes=[pltpu.VMEM((DEPTH,) + buf_shape, weight.dtype), pltpu.SemaphoreType.DMA((DEPTH,))],
        cost_estimate=pl.CostEstimate(flops=flops, bytes_accessed=nbytes, transcendentals=0),
    )(count, pair_tile, pair_block, dense, weight)


LINE_MAX = 4
CAPACITIES = (12, 14, 16, 18, 20, 22, 24)


def line_pairs(n, k, rightward):
    return [(i, i + k) if rightward else (i + k, i) for i in range(n - k)]


def line_gather(x, axis):
    n = lax.axis_size(axis)
    if n > LINE_MAX:
        return lax.all_gather(x, axis, axis=0, tiled=True)
    me = lax.axis_index(axis)
    parts = [x]
    sources = [me]
    for k in range(1, n):
        parts.append(lax.ppermute(x, axis, line_pairs(n, k, True)))
        sources.append(me - k)
        parts.append(lax.ppermute(x, axis, line_pairs(n, k, False)))
        sources.append(me + k)
    out = jnp.zeros((n,) + x.shape, x.dtype)
    for part, src in zip(parts, sources):
        ok = (src >= 0) & (src < n)
        out = lax.dynamic_update_index_in_dim(
            out, jnp.where(ok, part, out[jnp.clip(src, 0, n - 1)]), jnp.clip(src, 0, n - 1), 0
        )
    return out.reshape((n * x.shape[0],) + x.shape[1:])


def shift_gather(x, axis):
    n = lax.axis_size(axis)
    if n > LINE_MAX:
        return lax.all_gather(x, axis, axis=0, tiled=True)
    me = lax.axis_index(axis)
    out = jnp.zeros((n,) + x.shape, x.dtype)
    out = lax.dynamic_update_index_in_dim(out, x, me, 0)
    for k in range(1, n):
        got = lax.ppermute(x, axis, [(i, (i + k) % n) for i in range(n)])
        out = lax.dynamic_update_index_in_dim(out, got, (me - k) % n, 0)
    return out.reshape((n * x.shape[0],) + x.shape[1:])


def line_reduce_scatter(x, axis, wire):
    n = lax.axis_size(axis)
    if n > LINE_MAX or n & (n - 1):
        return lax.psum_scatter(x, axis, scatter_dimension=0, tiled=True)
    me = lax.axis_index(axis)
    rows = x.shape[0] // n
    bits = n.bit_length() - 1
    x = x.reshape((2,) * bits + (rows,) + x.shape[1:])
    for j in range(bits):
        level = 1 << j
        bit = (me // level) % 2
        keep = lax.dynamic_index_in_dim(x, bit, axis=bits - 1 - j, keepdims=False)
        send = lax.dynamic_index_in_dim(x, 1 - bit, axis=bits - 1 - j, keepdims=False).astype(wire)
        x = keep + lax.ppermute(send, axis, [(i, i ^ level) for i in range(n)]).astype(keep.dtype)
    return x


def halving_steps():
    steps = []
    for axis in ("section", "tok"):
        n = lax.axis_size(axis)
        if n & (n - 1):
            return None
        me = lax.axis_index(axis)
        level = n // 2
        while level:
            steps.append((axis, (me // level) % 2, [(i, i ^ level) for i in range(n)]))
            level //= 2
    return steps


def halving_sum(x, steps):
    for axis, bit, perm in steps:
        half = x.shape[1] // 2
        keep = lax.dynamic_slice_in_dim(x, bit * half, half, axis=1)
        send = lax.dynamic_slice_in_dim(x, (1 - bit) * half, half, axis=1)
        x = keep + lax.ppermute(send, axis, perm)
    return x


def doubling_gather(x, steps):
    for axis, bit, perm in reversed(steps):
        got = lax.ppermute(x, axis, perm)
        x = jnp.where(bit == 0, jnp.concatenate([x, got], axis=1), jnp.concatenate([got, x], axis=1))
    return x


def shards(acts, enc_weight, enc_bias, dec_weight, dec_bias, active_blocks, block_counts):
    local_enc = enc_weight[0]
    local_dec = dec_weight[:, 0, :]
    width, n_lat = local_enc.shape
    tokens_all = shift_gather(acts[0], "latent")
    n_tok = tokens_all.shape[0]
    tiles = n_tok // TILE
    blocks_local = n_lat // BLOCK
    most = tiles * min(active_blocks.shape[1], blocks_local)
    first_block = lax.axis_index("latent") * blocks_local

    def table(capacity):
        return pair_table(active_blocks, block_counts, first_block, blocks_local, capacity)

    def middle(capacity, pairs):
        pair_valid, count, pair_tile, pair_block = pairs
        compact = sparse_call(
            encode_kernel,
            jax.ShapeDtypeStruct((capacity, TILE, BLOCK), jnp.float32),
            (width, BLOCK),
            count, pair_tile, pair_block, tokens_all, local_enc,
            2 * capacity * TILE * width * BLOCK, capacity * (width * BLOCK * 2 + TILE * BLOCK * 4),
        )
        steps = halving_steps()
        if steps is None:
            shared = lax.psum_scatter(compact, ("section", "tok"), scatter_dimension=1, tiled=True)
        else:
            shared = halving_sum(compact, steps)
        bias_pairs = enc_bias.reshape(blocks_local, BLOCK)[pair_block]
        codes_part = jnp.where(
            pair_valid[:, None, None], jax.nn.relu(shared + bias_pairs[:, None, :]), 0.0
        ).astype(jnp.bfloat16)
        if steps is None:
            codes = lax.all_gather(codes_part, ("section", "tok"), axis=1, tiled=True)
        else:
            codes = doubling_gather(codes_part, steps)
        return sparse_call(
            decode_kernel,
            jax.ShapeDtypeStruct((n_tok, local_dec.shape[1]), jnp.float32),
            (BLOCK, local_dec.shape[1]),
            count, pair_tile, pair_block, codes, local_dec,
            2 * capacity * TILE * BLOCK * local_dec.shape[1], capacity * BLOCK * local_dec.shape[1] * 2,
        )

    levels = [c for c in CAPACITIES if c < most]
    if levels:
        listed = jnp.arange(active_blocks.shape[1], dtype=jnp.int32)[None, :] < block_counts[:, None]
        shard_of = active_blocks // blocks_local
        fullest = jnp.max(
            jnp.stack([jnp.sum((listed & (shard_of == s)).astype(jnp.int32)) for s in range(lax.axis_size("latent"))])
        )
        branch = sum((fullest > c).astype(jnp.int32) for c in levels)
        tables = [table(c) for c in levels + [most]]
        partial = lax.switch(branch, [functools.partial(middle, c, t) for c, t in zip(levels + [most], tables)])
    else:
        partial = middle(most, table(most))
    rebuilt = line_reduce_scatter(partial, "latent", jnp.bfloat16)
    return (rebuilt + dec_bias).astype(jnp.bfloat16)[None]


def solution(mesh):
    placed = (
        P("section", "latent", "tok"),
        P("section", "tok", "latent"),
        P("latent"),
        P("latent", "section", "tok"),
        P("section", "tok"),
        P(),
        P(),
    )
    return jax.shard_map(
        shards, mesh=mesh, in_specs=placed, out_specs=P("section", "latent", "tok"), check_vma=False
    )
```

```python
import functools

import jax
import jax.numpy as jnp
from jax import lax
from jax.experimental import pallas as pl
from jax.experimental.pallas import tpu as pltpu
from jax.sharding import PartitionSpec as P

BLOCK = 128
TILE = 128


def pair_table(active_blocks, block_counts, first_block, blocks_local, capacity):
    tiles, listed = active_blocks.shape
    slot_ids = jnp.arange(listed, dtype=jnp.int32)
    local = active_blocks - first_block
    valid = ((slot_ids[None, :] < block_counts[:, None]) & (local >= 0) & (local < blocks_local)).reshape(-1)
    order = jnp.argsort(jnp.logical_not(valid).astype(jnp.int32), stable=True)[:capacity].astype(jnp.int32)
    pair_valid = valid[order]
    pair_tile = order // listed
    pair_block = jnp.where(pair_valid, local.reshape(-1)[order], 0)
    count = jnp.minimum(jnp.sum(valid.astype(jnp.int32)), capacity).reshape(1)
    return pair_valid, count, pair_tile, pair_block


DEPTH = 10


def weight_stream(n, blk_ref, source, buf, sem, compute):
    def copy(i, slot):
        return pltpu.make_async_copy(source(blk_ref[i]), buf.at[slot], sem.at[slot])

    for j in range(DEPTH):
        @pl.when(j < n)
        def _():
            copy(j, j).start()

    def body(i, carry):
        slot = i % DEPTH
        copy(i, slot).wait()
        compute(i, buf.at[slot])

        @pl.when(i + DEPTH < n)
        def _():
            copy(i + DEPTH, slot).start()

        return carry

    lax.fori_loop(0, n, body, 0)


def encode_kernel(n_ref, tile_ref, blk_ref, acts_ref, enc_hbm, out_ref, buf, sem):

    def source(b):
        return enc_hbm.at[:, pl.ds(pl.multiple_of(b * BLOCK, BLOCK), BLOCK)]

    def compute(i, block):
        rows = acts_ref[pl.ds(pl.multiple_of(tile_ref[i] * TILE, TILE), TILE), :]
        out_ref[i] = jnp.dot(rows, block[...], preferred_element_type=jnp.float32)

    weight_stream(n_ref[0], blk_ref, source, buf, sem, compute)


def decode_kernel(n_ref, tile_ref, blk_ref, codes_ref, dec_hbm, out_ref, buf, sem):
    out_ref[...] = jnp.zeros(out_ref.shape, out_ref.dtype)

    def source(b):
        return dec_hbm.at[pl.ds(pl.multiple_of(b * BLOCK, BLOCK), BLOCK), :]

    def compute(i, block):
        rows = pl.ds(pl.multiple_of(tile_ref[i] * TILE, TILE), TILE)
        out_ref[rows, :] += jnp.dot(codes_ref[i], block[...], preferred_element_type=jnp.float32)

    weight_stream(n_ref[0], blk_ref, source, buf, sem, compute)


def sparse_call(kernel, out_shape, buf_shape, count, pair_tile, pair_block, dense, weight, flops, nbytes):
    smem = pl.BlockSpec(memory_space=pltpu.SMEM)
    return pl.pallas_call(
        kernel,
        out_shape=out_shape,
        in_specs=[smem, smem, smem, pl.BlockSpec(memory_space=pltpu.VMEM), pl.BlockSpec(memory_space=pl.ANY)],
        out_specs=pl.BlockSpec(memory_space=pltpu.VMEM),
        scratch_shapes=[pltpu.VMEM((DEPTH,) + buf_shape, weight.dtype), pltpu.SemaphoreType.DMA((DEPTH,))],
        cost_estimate=pl.CostEstimate(flops=flops, bytes_accessed=nbytes, transcendentals=0),
    )(count, pair_tile, pair_block, dense, weight)


LINE_MAX = 4
CAPACITIES = (12, 13, 14, 15, 16, 17, 18, 20, 22, 24)


def line_pairs(n, k, rightward):
    return [(i, i + k) if rightward else (i + k, i) for i in range(n - k)]


def line_gather(x, axis):
    n = lax.axis_size(axis)
    if n > LINE_MAX:
        return lax.all_gather(x, axis, axis=0, tiled=True)
    me = lax.axis_index(axis)
    parts = [x]
    sources = [me]
    for k in range(1, n):
        parts.append(lax.ppermute(x, axis, line_pairs(n, k, True)))
        sources.append(me - k)
        parts.append(lax.ppermute(x, axis, line_pairs(n, k, False)))
        sources.append(me + k)
    out = jnp.zeros((n,) + x.shape, x.dtype)
    for part, src in zip(parts, sources):
        ok = (src >= 0) & (src < n)
        out = lax.dynamic_update_index_in_dim(
            out, jnp.where(ok, part, out[jnp.clip(src, 0, n - 1)]), jnp.clip(src, 0, n - 1), 0
        )
    return out.reshape((n * x.shape[0],) + x.shape[1:])


def shift_gather(x, axis):
    n = lax.axis_size(axis)
    if n > LINE_MAX:
        return lax.all_gather(x, axis, axis=0, tiled=True)
    me = lax.axis_index(axis)
    out = jnp.zeros((n,) + x.shape, x.dtype)
    out = lax.dynamic_update_index_in_dim(out, x, me, 0)
    for k in range(1, n):
        got = lax.ppermute(x, axis, [(i, (i + k) % n) for i in range(n)])
        out = lax.dynamic_update_index_in_dim(out, got, (me - k) % n, 0)
    return out.reshape((n * x.shape[0],) + x.shape[1:])


def line_reduce_scatter(x, axis, wire):
    n = lax.axis_size(axis)
    if n > LINE_MAX or n & (n - 1):
        return lax.psum_scatter(x, axis, scatter_dimension=0, tiled=True)
    me = lax.axis_index(axis)
    rows = x.shape[0] // n
    bits = n.bit_length() - 1
    x = x.reshape((2,) * bits + (rows,) + x.shape[1:])
    for j in range(bits):
        level = 1 << j
        bit = (me // level) % 2
        keep = lax.dynamic_index_in_dim(x, bit, axis=bits - 1 - j, keepdims=False)
        send = lax.dynamic_index_in_dim(x, 1 - bit, axis=bits - 1 - j, keepdims=False).astype(wire)
        x = keep + lax.ppermute(send, axis, [(i, i ^ level) for i in range(n)]).astype(keep.dtype)
    return x


def halving_steps():
    steps = []
    for axis in ("section", "tok"):
        n = lax.axis_size(axis)
        if n & (n - 1):
            return None
        me = lax.axis_index(axis)
        level = n // 2
        while level:
            steps.append((axis, (me // level) % 2, [(i, i ^ level) for i in range(n)]))
            level //= 2
    return steps


def halving_sum(x, steps):
    for axis, bit, perm in steps:
        half = x.shape[1] // 2
        keep = lax.dynamic_slice_in_dim(x, bit * half, half, axis=1)
        send = lax.dynamic_slice_in_dim(x, (1 - bit) * half, half, axis=1)
        x = keep + lax.ppermute(send, axis, perm)
    return x


def doubling_gather(x, steps):
    for axis, bit, perm in reversed(steps):
        got = lax.ppermute(x, axis, perm)
        x = jnp.where(bit == 0, jnp.concatenate([x, got], axis=1), jnp.concatenate([got, x], axis=1))
    return x


def shards(acts, enc_weight, enc_bias, dec_weight, dec_bias, active_blocks, block_counts):
    local_enc = enc_weight[0]
    local_dec = dec_weight[:, 0, :]
    width, n_lat = local_enc.shape
    tokens_all = shift_gather(acts[0], "latent")
    n_tok = tokens_all.shape[0]
    tiles = n_tok // TILE
    blocks_local = n_lat // BLOCK
    most = tiles * min(active_blocks.shape[1], blocks_local)
    first_block = lax.axis_index("latent") * blocks_local

    def table(capacity):
        return pair_table(active_blocks, block_counts, first_block, blocks_local, capacity)

    def middle(capacity, pairs):
        pair_valid, count, pair_tile, pair_block = pairs
        compact = sparse_call(
            encode_kernel,
            jax.ShapeDtypeStruct((capacity, TILE, BLOCK), jnp.float32),
            (width, BLOCK),
            count, pair_tile, pair_block, tokens_all, local_enc,
            2 * capacity * TILE * width * BLOCK, capacity * (width * BLOCK * 2 + TILE * BLOCK * 4),
        )
        steps = halving_steps()
        if steps is None:
            shared = lax.psum_scatter(compact, ("section", "tok"), scatter_dimension=1, tiled=True)
        else:
            shared = halving_sum(compact, steps)
        bias_pairs = enc_bias.reshape(blocks_local, BLOCK)[pair_block]
        codes_part = jnp.where(
            pair_valid[:, None, None], jax.nn.relu(shared + bias_pairs[:, None, :]), 0.0
        ).astype(jnp.bfloat16)
        if steps is None:
            codes = lax.all_gather(codes_part, ("section", "tok"), axis=1, tiled=True)
        else:
            codes = doubling_gather(codes_part, steps)
        return sparse_call(
            decode_kernel,
            jax.ShapeDtypeStruct((n_tok, local_dec.shape[1]), jnp.float32),
            (BLOCK, local_dec.shape[1]),
            count, pair_tile, pair_block, codes, local_dec,
            2 * capacity * TILE * BLOCK * local_dec.shape[1], capacity * BLOCK * local_dec.shape[1] * 2,
        )

    levels = [c for c in CAPACITIES if c < most]
    if levels:
        listed = jnp.arange(active_blocks.shape[1], dtype=jnp.int32)[None, :] < block_counts[:, None]
        shard_of = active_blocks // blocks_local
        fullest = jnp.max(
            jnp.stack([jnp.sum((listed & (shard_of == s)).astype(jnp.int32)) for s in range(lax.axis_size("latent"))])
        )
        branch = sum((fullest > c).astype(jnp.int32) for c in levels)
        tables = [table(c) for c in levels + [most]]
        partial = lax.switch(branch, [functools.partial(middle, c, t) for c, t in zip(levels + [most], tables)])
    else:
        partial = middle(most, table(most))
    rebuilt = line_reduce_scatter(partial, "latent", jnp.bfloat16)
    return (rebuilt + dec_bias).astype(jnp.bfloat16)[None]


def solution(mesh):
    placed = (
        P("section", "latent", "tok"),
        P("section", "tok", "latent"),
        P("latent"),
        P("latent", "section", "tok"),
        P("section", "tok"),
        P(),
        P(),
    )
    return jax.shard_map(
        shards, mesh=mesh, in_specs=placed, out_specs=P("section", "latent", "tok"), check_vma=False
    )
```
